32 devices in a mesh: groups: 2 (over y), cent: 4 (over z), dp: 2 (over x), sub: 2 (over core).
Axes of the slice: x: 2, y: 2, z: 4, core: 2. Of those that a mesh axis runs over, the one named last changes fastest.
Arguments:
- embeddings: bfloat16 [1024, 768], P(('groups', 'cent', 'dp', 'sub')), parts along dimension 0, may hold values from -6 to 6
- weights: int32 [1024], P(('groups', 'cent', 'dp', 'sub')), parts along dimension 0, may hold values from 1 to 4
- centroids: bfloat16 [16384, 768], P(('groups', 'cent')), parts along dimension 0, may hold values from -6 to 6
- inverse_temp: float32 [1], replicated, may hold values from 16 to 256
Outputs:
- centroid_sums: float32 [16384, 768], P(('groups', 'cent', 'dp', 'sub')), parts along dimension 0
- renormed: bfloat16 [16384, 768], P(('groups', 'cent', 'dp', 'sub')), parts along dimension 0
- objective: float32 [1024], P(('groups', 'cent', 'dp', 'sub')), parts along dimension 0
The draws below stay inside these ranges and needn't reach their ends.
There are 2 independent parts, one for each index of `groups`. The reference program is written for one: setup_inputs(seed, part) draws one part's arguments, and reference() takes and returns one part's arrays. A program takes and returns all parts, laid end to end along the dimension named above; an argument that names none is the same for every part. Nothing has to cross between parts.
All inputs are finite; a program needn't handle non-finite values.
Results may differ from the reference program's by a relative error of at most 0.0075.
The reference program's roundings to bfloat16 on the way (of `unit_rows`, `unit_cents` and `responsibility`) count: a program that leaves them out, or rounds other values in their place, can miss the bound.
Values may be sent and summed in bfloat16 or wider, within the bound.
No kernel may reach another device: no remote copies, remote signals or barrier semaphores. Data moves between devices by JAX's collectives and lax.ppermute only.
A program may use at most 64 MiB of HBM per device.

```python
import jax
import jax.numpy as jnp
from jax import lax

D = 768
ROW_DEV = 32
K = 8192
ROWS = 512
N_CENT = 4
N_DP = 2
N_SUB = 2


def topic_table(key):
    topic_count = max(K // 1024, 4)
    topics = jax.random.normal(jax.random.fold_in(key, 31), (topic_count, D), jnp.float32)
    return (topics, topic_count)


def centroid_values(key):
    topics, topic_count = topic_table(key)
    cent_topic = jax.random.randint(jax.random.fold_in(key, 13), (K,), 0, topic_count)
    values = jax.random.normal(jax.random.fold_in(key, 11), (K, D), jnp.float32) + topics[cent_topic]
    return jnp.clip(values, -6.0, 6.0)


def draw_centroids(key, part):
    return centroid_values(key).astype(jnp.bfloat16)


def draw_embeddings(key, part):
    topics, topic_count = topic_table(key)
    row_topic = jax.random.randint(jax.random.fold_in(key, 26), (ROWS,), 0, topic_count)
    strength = jax.random.uniform(jax.random.fold_in(key, 27), (ROWS, 1), jnp.float32, 0.3, 1.5)
    noise = jax.random.normal(jax.random.fold_in(key, 21), (ROWS, D), jnp.float32)
    embedding_rows = noise + strength * topics[row_topic]
    return jnp.clip(embedding_rows, -6.0, 6.0).astype(jnp.bfloat16)


def draw_inverse_temp(key, part):
    value = jax.random.uniform(jax.random.fold_in(key, 41), (1,), jnp.float32, 16.0, 32.0)
    return value


def with_ends(values, stream_key, smallest, largest):
    shape = values.shape
    place = [jax.random.randint(jax.random.fold_in(stream_key, axis), (), 0, shape[axis]) for axis in range(len(shape))]
    values = values.at[tuple(place)].set(smallest)
    longest = shape.index(max(shape))
    place[longest] = (place[longest] + 1) % shape[longest]
    return values.at[tuple(place)].set(largest)


def setup_inputs(seed: int = 0, part: int = 0) -> dict:
    splits = jax.random.split(jax.random.key(seed), 5)
    own_keys = jax.random.split(jax.random.fold_in(splits[4], part), 5)
    embeddings = draw_embeddings(jax.random.fold_in(jax.random.fold_in(splits[4], part), 71), part)
    weights = with_ends(jax.random.randint(own_keys[1], (ROWS,), 1, 5), jax.random.fold_in(own_keys[1], 1), 1, 4).astype(jnp.int32)
    centroids = draw_centroids(jax.random.fold_in(jax.random.fold_in(splits[4], part), 71), part)
    inverse_temp = draw_inverse_temp(jax.random.fold_in(splits[4], 71), part)
    return dict(embeddings=embeddings, weights=weights, centroids=centroids, inverse_temp=inverse_temp)


def normalize(values):
    floats = values.astype(jnp.float32)
    return (floats * lax.rsqrt(lax.optimization_barrier(jnp.sum(floats * floats, axis=-1, keepdims=True)) + 1e-06)).astype(jnp.bfloat16)

def reference(embeddings, weights, centroids, inverse_temp):
    sharpness = inverse_temp[0]
    unit_rows = normalize(embeddings)
    unit_cents = normalize(centroids)
    row_groups = N_DP * N_SUB
    grouped_rows = unit_rows.reshape(N_CENT, row_groups, ROW_DEV, D).transpose(1, 0, 2, 3).reshape(row_groups, N_CENT * ROW_DEV, D)
    grouped_weights = weights.reshape(N_CENT, row_groups, ROW_DEV).transpose(1, 0, 2).reshape(row_groups, N_CENT * ROW_DEV)

    def one_group(carry, inputs):
        sums_acc, mass_acc = carry
        block_rows, block_weights = inputs
        scores = jnp.dot(block_rows, unit_cents.T, preferred_element_type=jnp.float32) * sharpness
        row_peak = lax.optimization_barrier(jnp.max(scores, axis=1, keepdims=True))
        row_total = lax.optimization_barrier(jnp.sum(jnp.exp(scores - row_peak), axis=1, keepdims=True))
        log_sum = row_peak + jnp.log(row_total)
        weight_float = block_weights.astype(jnp.float32)[:, None]
        responsibility = (weight_float * jnp.exp(scores - log_sum)).astype(jnp.bfloat16)
        partial_value = jnp.dot(responsibility.T, block_rows, preferred_element_type=jnp.float32).astype(jnp.bfloat16)
        weight_mass = lax.optimization_barrier(jnp.sum(responsibility.astype(jnp.float32), axis=0)).astype(jnp.bfloat16)
        carry = (sums_acc + partial_value.astype(jnp.float32), mass_acc + weight_mass.astype(jnp.float32))
        return (carry, (weight_float * log_sum)[:, 0] / sharpness)
    start = (jnp.zeros((K, D), jnp.float32), jnp.zeros((K,), jnp.float32))
    (centroid_sums, mass), grouped_objective = lax.scan(one_group, start, (grouped_rows, grouped_weights))
    objective = grouped_objective.reshape(row_groups, N_CENT, ROW_DEV).transpose(1, 0, 2).reshape(ROWS)
    moved = unit_cents.astype(jnp.float32) + centroid_sums / (mass + 1.0)[:, None]
    renormed = (moved * lax.rsqrt(lax.optimization_barrier(jnp.sum(moved * moved, axis=-1, keepdims=True)) + 1e-06)).astype(jnp.bfloat16)
    return (centroid_sums, renormed, objective)
```

```python
import jax
import jax.numpy as jnp
from jax import lax
from jax.sharding import PartitionSpec as P

PART_AXES = ("cent", "dp", "sub")


def normalize(values):
    floats = values.astype(jnp.float32)
    return floats * lax.rsqrt(jnp.sum(floats * floats, axis=-1, keepdims=True) + 1e-06)


def merged_log_sum(local_peak, local_total):
    stats = jnp.stack([local_peak, local_total])
    if stats.size * 4 * lax.axis_size(PART_AXES) <= (8 << 20):
        gathered = lax.all_gather(stats, PART_AXES, axis=0)
        peaks, totals = gathered[:, 0], gathered[:, 1]
        row_peak = jnp.max(peaks, axis=0)
        row_total = jnp.sum(totals * jnp.exp(peaks - row_peak[None, :]), axis=0)
    else:
        row_peak = lax.pmax(local_peak, PART_AXES)
        row_total = lax.psum(local_total * jnp.exp(local_peak - row_peak), PART_AXES)
    return row_peak + jnp.log(row_total)


def shards(embeddings, weights, centroids, inverse_temp):
    sharpness = inverse_temp[0]
    row_dev, width = embeddings.shape
    n_cent = lax.axis_size("cent")
    n_groups = lax.axis_size(("dp", "sub"))
    own_count = centroids.shape[0] // n_groups

    weight_cols = jnp.broadcast_to(weights.astype(jnp.bfloat16)[:, None], (row_dev, 128))
    packed = jnp.concatenate([embeddings, weight_cols], axis=1)
    gathered = lax.all_gather(packed, PART_AXES, axis=0, tiled=True)
    unit_rows = normalize(gathered[:, :width]).astype(jnp.bfloat16)
    weight_float = gathered[:, width].astype(jnp.float32)

    offset = lax.axis_index(("dp", "sub")) * own_count
    own_cents = normalize(lax.dynamic_slice_in_dim(centroids, offset, own_count, 0)).astype(jnp.bfloat16)

    scores = (
        lax.dot_general(
            unit_rows, own_cents, (((1,), (1,)), ((), ())), preferred_element_type=jnp.float32
        )
        * sharpness
    )
    local_peak = jnp.max(scores, axis=1)
    local_total = jnp.sum(jnp.exp(scores - local_peak[:, None]), axis=1)
    log_sum = merged_log_sum(local_peak, local_total)

    responsibility = (weight_float[:, None] * jnp.exp(scores - log_sum[:, None])).astype(jnp.bfloat16)
    grouped_resp = responsibility.reshape(n_cent, n_groups, row_dev, own_count)
    grouped_rows = unit_rows.reshape(n_cent, n_groups, row_dev, width)
    partial_value = lax.dot_general(
        grouped_resp,
        grouped_rows,
        (((0, 2), (0, 2)), ((1,), (1,))),
        preferred_element_type=jnp.float32,
    ).astype(jnp.bfloat16)
    centroid_sums = jnp.sum(partial_value.astype(jnp.float32), axis=0)
    weight_mass = jnp.sum(grouped_resp.astype(jnp.float32), axis=(0, 2)).astype(jnp.bfloat16)
    own_mass = jnp.sum(weight_mass.astype(jnp.float32), axis=0)

    moved = own_cents.astype(jnp.float32) + centroid_sums / (own_mass + 1.0)[:, None]
    renormed = normalize(moved).astype(jnp.bfloat16)

    row_offset = lax.axis_index(PART_AXES) * row_dev
    weighted_log_sum = weight_float * log_sum / sharpness
    objective = lax.dynamic_slice_in_dim(weighted_log_sum, row_offset, row_dev, 0)
    return (centroid_sums, renormed, objective)


def solution(mesh):
    in_specs = (
        P(("groups", "cent", "dp", "sub"), None),
        P(("groups", "cent", "dp", "sub")),
        P(("groups", "cent"), None),
        P(),
    )
    out_specs = (
        P(("groups", "cent", "dp", "sub"), None),
        P(("groups", "cent", "dp", "sub"), None),
        P(("groups", "cent", "dp", "sub")),
    )
    return jax.shard_map(shards, mesh=mesh, in_specs=in_specs, out_specs=out_specs, check_vma=False)
```

```python
import jax
import jax.numpy as jnp
from jax import lax
from jax.sharding import PartitionSpec as P

STAGES = ("cent", "dp", "sub")
SHIFT_MAX = 4


def normalize(values):
    floats = values.astype(jnp.float32)
    return floats * lax.rsqrt(jnp.sum(floats * floats, axis=-1, keepdims=True) + 1e-06)


def relative(name):
    return lax.axis_size(name) <= SHIFT_MAX


def gather_stage(value, name):
    size = lax.axis_size(name)
    if relative(name):
        parts = [value] + [
            lax.ppermute(value, name, [(j, (j + q) % size) for j in range(size)]) for q in range(1, size)
        ]
        return jnp.stack(parts)
    return lax.all_gather(value, name, axis=0)


def own_block(name):
    return 0 if relative(name) else lax.axis_index(name)


def shards(embeddings, weights, centroids, inverse_temp):
    sharpness = inverse_temp[0]
    row_dev, width = embeddings.shape
    sizes = {name: lax.axis_size(name) for name in STAGES}
    n_groups = sizes["dp"] * sizes["sub"]
    own_count = centroids.shape[0] // n_groups

    weight_cols = jnp.broadcast_to(weights.astype(jnp.bfloat16)[:, None], (row_dev, 128))
    blocks = jnp.concatenate([embeddings, weight_cols], axis=1)
    for name in STAGES:
        blocks = gather_stage(blocks, name)
    gathered = blocks.reshape(-1, width + 128)
    unit_rows = normalize(gathered[:, :width]).astype(jnp.bfloat16)
    weight_float = gathered[:, width].astype(jnp.float32)

    offset = lax.axis_index(("dp", "sub")) * own_count
    own_cents = normalize(lax.dynamic_slice_in_dim(centroids, offset, own_count, 0)).astype(jnp.bfloat16)

    scores = (
        lax.dot_general(
            unit_rows, own_cents, (((1,), (1,)), ((), ())), preferred_element_type=jnp.float32
        )
        * sharpness
    )
    block_shape = (sizes["sub"], sizes["dp"], sizes["cent"], row_dev)
    local_peak = jnp.max(scores, axis=1)
    local_total = jnp.sum(jnp.exp(scores - local_peak[:, None]), axis=1)

    stats = jnp.stack([local_peak.reshape(block_shape), local_total.reshape(block_shape)])
    block_axis = {"sub": 1, "dp": 2, "cent": 3}
    for name in STAGES:
        stacked = gather_stage(stats, name)
        if relative(name):
            stacked = jnp.stack(
                [jnp.roll(stacked[q], q, axis=block_axis[name]) for q in range(sizes[name])]
            )
        peaks, totals = stacked[:, 0], stacked[:, 1]
        row_peak = jnp.max(peaks, axis=0)
        row_total = jnp.sum(totals * jnp.exp(peaks - row_peak[None]), axis=0)
        stats = jnp.stack([row_peak, row_total])
    log_sum = (stats[0] + jnp.log(stats[1])).reshape(-1)

    responsibility = (weight_float[:, None] * jnp.exp(scores - log_sum[:, None])).astype(jnp.bfloat16)
    grouped_resp = responsibility.reshape(n_groups, -1, own_count)
    grouped_rows = unit_rows.reshape(n_groups, -1, width)
    partial_value = lax.dot_general(
        grouped_resp, grouped_rows, (((1,), (1,)), ((0,), (0,))), preferred_element_type=jnp.float32
    ).astype(jnp.bfloat16)
    centroid_sums = jnp.sum(partial_value.astype(jnp.float32), axis=0)
    weight_mass = jnp.sum(grouped_resp.astype(jnp.float32), axis=1).astype(jnp.bfloat16)
    own_mass = jnp.sum(weight_mass.astype(jnp.float32), axis=0)

    moved = own_cents.astype(jnp.float32) + centroid_sums / (own_mass + 1.0)[:, None]
    renormed = normalize(moved).astype(jnp.bfloat16)

    weighted_log_sum = (weight_float * log_sum / sharpness).reshape(block_shape)
    objective = weighted_log_sum[own_block("sub"), own_block("dp"), own_block("cent")]
    return (centroid_sums, renormed, objective)


def solution(mesh):
    in_specs = (
        P(("groups", "cent", "dp", "sub"), None),
        P(("groups", "cent", "dp", "sub")),
        P(("groups", "cent"), None),
        P(),
    )
    out_specs = (
        P(("groups", "cent", "dp", "sub"), None),
        P(("groups", "cent", "dp", "sub"), None),
        P(("groups", "cent", "dp", "sub")),
    )
    return jax.shard_map(shards, mesh=mesh, in_specs=in_specs, out_specs=out_specs, check_vma=False)
```

```python
import jax
import jax.numpy as jnp
from jax import lax
from jax.sharding import PartitionSpec as P

STAGES = ("cent", "dp", "sub")
SHIFT_MAX = 4


def normalize(values):
    floats = values.astype(jnp.float32)
    return floats * lax.rsqrt(jnp.sum(floats * floats, axis=-1, keepdims=True) + 1e-06)


def relative(name):
    return lax.axis_size(name) <= SHIFT_MAX


def gather_stage(value, name):
    size = lax.axis_size(name)
    if relative(name):
        parts = [value] + [
            lax.ppermute(value, name, [(j, (j + q) % size) for j in range(size)]) for q in range(1, size)
        ]
        return jnp.stack(parts)
    return lax.all_gather(value, name, axis=0)


def own_block(name):
    return 0 if relative(name) else lax.axis_index(name)


def shards(embeddings, weights, centroids, inverse_temp):
    sharpness = inverse_temp[0]
    row_dev, width = embeddings.shape
    sizes = {name: lax.axis_size(name) for name in STAGES}
    n_groups = sizes["dp"] * sizes["sub"]
    own_count = centroids.shape[0] // n_groups

    blocks = embeddings
    for name in STAGES:
        blocks = gather_stage(blocks, name)
    unit_rows = normalize(blocks.reshape(-1, width)).astype(jnp.bfloat16)

    offset = lax.axis_index(("dp", "sub")) * own_count
    own_cents = normalize(lax.dynamic_slice_in_dim(centroids, offset, own_count, 0)).astype(jnp.bfloat16)
    own_cents = lax.optimization_barrier(own_cents)

    scores = (
        lax.dot_general(
            unit_rows, own_cents, (((1,), (1,)), ((), ())), preferred_element_type=jnp.float32
        )
        * sharpness
    )
    block_shape = (sizes["sub"], sizes["dp"], sizes["cent"], row_dev)
    local_peak = jnp.max(scores, axis=1)
    local_total = jnp.sum(jnp.exp(scores - local_peak[:, None]), axis=1)

    own_index = (own_block("sub"), own_block("dp"), own_block("cent"), 0)
    known_weights = lax.dynamic_update_slice(
        jnp.zeros(block_shape, jnp.float32), weights.astype(jnp.float32)[None, None, None], own_index
    )
    stats = jnp.stack([local_peak.reshape(block_shape), local_total.reshape(block_shape), known_weights])
    block_axis = {"sub": 1, "dp": 2, "cent": 3}
    for name in STAGES:
        stacked = gather_stage(stats, name)
        if relative(name):
            stacked = jnp.stack(
                [jnp.roll(stacked[q], q, axis=block_axis[name]) for q in range(sizes[name])]
            )
        peaks, totals = stacked[:, 0], stacked[:, 1]
        row_peak = jnp.max(peaks, axis=0)
        row_total = jnp.sum(totals * jnp.exp(peaks - row_peak[None]), axis=0)
        stats = jnp.stack([row_peak, row_total, jnp.sum(stacked[:, 2], axis=0)])
    weight_float = stats[2].reshape(-1)
    log_sum = (stats[0] + jnp.log(stats[1])).reshape(-1)

    responsibility = (weight_float[:, None] * jnp.exp(scores - log_sum[:, None])).astype(jnp.bfloat16)
    grouped_resp = responsibility.reshape(n_groups, -1, own_count)
    grouped_rows = unit_rows.reshape(n_groups, -1, width)
    partial_value = lax.dot_general(
        grouped_resp, grouped_rows, (((1,), (1,)), ((0,), (0,))), preferred_element_type=jnp.float32
    ).astype(jnp.bfloat16)
    centroid_sums = jnp.sum(partial_value.astype(jnp.float32), axis=0)
    weight_mass = jnp.sum(grouped_resp.astype(jnp.float32), axis=1).astype(jnp.bfloat16)
    own_mass = jnp.sum(weight_mass.astype(jnp.float32), axis=0)

    moved = own_cents.astype(jnp.float32) + centroid_sums / (own_mass + 1.0)[:, None]
    renormed = normalize(moved).astype(jnp.bfloat16)

    own_log_sum = log_sum.reshape(block_shape)[own_index[:3]]
    objective = weights.astype(jnp.float32) * own_log_sum / sharpness
    return (centroid_sums, renormed, objective)


def solution(mesh):
    in_specs = (
        P(("groups", "cent", "dp", "sub"), None),
        P(("groups", "cent", "dp", "sub")),
        P(("groups", "cent"), None),
        P(),
    )
    out_specs = (
        P(("groups", "cent", "dp", "sub"), None),
        P(("groups", "cent", "dp", "sub"), None),
        P(("groups", "cent", "dp", "sub")),
    )
    return jax.shard_map(shards, mesh=mesh, in_specs=in_specs, out_specs=out_specs, check_vma=False)
```

```python
import jax
import jax.numpy as jnp
from jax import lax
from jax.sharding import PartitionSpec as P

STAGES = ("cent", ("dp", "sub"))
SHIFT_MAX = 4


def normalize(values):
    floats = values.astype(jnp.float32)
    return floats * lax.rsqrt(jnp.sum(floats * floats, axis=-1, keepdims=True) + 1e-06)


def relative(name):
    return lax.axis_size(name) <= SHIFT_MAX


def gather_stage(value, name):
    size = lax.axis_size(name)
    if relative(name):
        parts = [value] + [
            lax.ppermute(value, name, [(j, (j + q) % size) for j in range(size)]) for q in range(1, size)
        ]
        return jnp.stack(parts)
    return lax.all_gather(value, name, axis=0)


def own_block(name):
    return 0 if relative(name) else lax.axis_index(name)


def shards(embeddings, weights, centroids, inverse_temp):
    sharpness = inverse_temp[0]
    row_dev, width = embeddings.shape
    sizes = {name: lax.axis_size(name) for name in STAGES}
    n_groups = sizes[STAGES[1]]
    own_count = centroids.shape[0] // n_groups

    blocks = embeddings
    for name in STAGES:
        blocks = gather_stage(blocks, name)
    unit_rows = normalize(blocks.reshape(-1, width)).astype(jnp.bfloat16)

    offset = lax.axis_index(("dp", "sub")) * own_count
    own_cents = normalize(lax.dynamic_slice_in_dim(centroids, offset, own_count, 0)).astype(jnp.bfloat16)
    own_cents = lax.optimization_barrier(own_cents)

    scores = (
        lax.dot_general(
            unit_rows, own_cents, (((1,), (1,)), ((), ())), preferred_element_type=jnp.float32
        )
        * sharpness
    )
    block_shape = (n_groups, sizes["cent"], row_dev)
    local_peak = jnp.max(scores, axis=1)
    local_total = jnp.sum(jnp.exp(scores - local_peak[:, None]), axis=1)

    own_index = (own_block(STAGES[1]), own_block("cent"), 0)
    known_weights = lax.dynamic_update_slice(
        jnp.zeros(block_shape, jnp.float32), weights.astype(jnp.float32)[None, None], own_index
    )
    stats = jnp.stack([local_peak.reshape(block_shape), local_total.reshape(block_shape), known_weights])
    block_axis = {STAGES[1]: 1, "cent": 2}
    for name in STAGES:
        stacked = gather_stage(stats, name)
        if relative(name):
            stacked = jnp.stack(
                [jnp.roll(stacked[q], q, axis=block_axis[name]) for q in range(sizes[name])]
            )
        peaks, totals = stacked[:, 0], stacked[:, 1]
        row_peak = jnp.max(peaks, axis=0)
        row_total = jnp.sum(totals * jnp.exp(peaks - row_peak[None]), axis=0)
        stats = jnp.stack([row_peak, row_total, jnp.sum(stacked[:, 2], axis=0)])
    weight_float = stats[2].reshape(-1)
    log_sum = (stats[0] + jnp.log(stats[1])).reshape(-1)

    responsibility = (weight_float[:, None] * jnp.exp(scores - log_sum[:, None])).astype(jnp.bfloat16)
    grouped_resp = responsibility.reshape(n_groups, -1, own_count)
    grouped_rows = unit_rows.reshape(n_groups, -1, width)
    partial_value = lax.dot_general(
        grouped_resp, grouped_rows, (((1,), (1,)), ((0,), (0,))), preferred_element_type=jnp.float32
    ).astype(jnp.bfloat16)
    centroid_sums = jnp.sum(partial_value.astype(jnp.float32), axis=0)
    weight_mass = jnp.sum(grouped_resp.astype(jnp.float32), axis=1).astype(jnp.bfloat16)
    own_mass = jnp.sum(weight_mass.astype(jnp.float32), axis=0)

    moved = own_cents.astype(jnp.float32) + centroid_sums / (own_mass + 1.0)[:, None]
    renormed = normalize(moved).astype(jnp.bfloat16)

    own_log_sum = log_sum.reshape(block_shape)[own_index[:2]]
    objective = weights.astype(jnp.float32) * own_log_sum / sharpness
    return (centroid_sums, renormed, objective)


def solution(mesh):
    in_specs = (
        P(("groups", "cent", "dp", "sub"), None),
        P(("groups", "cent", "dp", "sub")),
        P(("groups", "cent"), None),
        P(),
    )
    out_specs = (
        P(("groups", "cent", "dp", "sub"), None),
        P(("groups", "cent", "dp", "sub"), None),
        P(("groups", "cent", "dp", "sub")),
    )
    return jax.shard_map(shards, mesh=mesh, in_specs=in_specs, out_specs=out_specs, check_vma=False)
```

```python
import jax
import jax.numpy as jnp
from jax import lax
from jax.sharding import PartitionSpec as P

PART_AXES = ("cent", "dp", "sub")


def normalize(values):
    floats = values.astype(jnp.float32)
    return floats * lax.rsqrt(jnp.sum(floats * floats, axis=-1, keepdims=True) + 1e-06)


def exchange_stages():
    stages = []
    for name in PART_AXES:
        size = lax.axis_size(name)
        if size & (size - 1):
            stages.append((name, 0))
            continue
        mask = 1
        while mask < size:
            stages.append((name, mask))
            mask *= 2
    return stages


def gather_stage(value, stage):
    name, mask = stage
    size = lax.axis_size(name)
    if mask:
        return jnp.stack([value, lax.ppermute(value, name, [(j, j ^ mask) for j in range(size)])])
    return lax.all_gather(value, name, axis=0)


def own_block(stage):
    name, mask = stage
    return 0 if mask else lax.axis_index(name)


def shards(embeddings, weights, centroids, inverse_temp):
    sharpness = inverse_temp[0]
    row_dev, width = embeddings.shape
    stages = exchange_stages()
    n_groups = lax.axis_size(("dp", "sub"))
    own_count = centroids.shape[0] // n_groups

    blocks = embeddings
    for stage in stages:
        blocks = gather_stage(blocks, stage)
    unit_rows = normalize(blocks.reshape(-1, width)).astype(jnp.bfloat16)

    offset = lax.axis_index(("dp", "sub")) * own_count
    own_cents = normalize(lax.dynamic_slice_in_dim(centroids, offset, own_count, 0)).astype(jnp.bfloat16)
    own_cents = lax.optimization_barrier(own_cents)

    scores = (
        lax.dot_general(
            unit_rows, own_cents, (((1,), (1,)), ((), ())), preferred_element_type=jnp.float32
        )
        * sharpness
    )
    block_shape = blocks.shape[:-1]
    local_peak = jnp.max(scores, axis=1)
    local_total = jnp.sum(jnp.exp(scores - local_peak[:, None]), axis=1)

    own_index = tuple(own_block(stage) for stage in reversed(stages)) + (0,)
    known_weights = lax.dynamic_update_slice(
        jnp.zeros(block_shape, jnp.float32), weights.astype(jnp.float32).reshape((1,) * len(stages) + (row_dev,)), own_index
    )
    stats = jnp.stack([local_peak.reshape(block_shape), local_total.reshape(block_shape), known_weights])
    for index, stage in enumerate(stages):
        stacked = gather_stage(stats, stage)
        if stage[1]:
            stacked = jnp.stack([stacked[0], jnp.flip(stacked[1], axis=len(stages) - index)])
        peaks, totals = stacked[:, 0], stacked[:, 1]
        row_peak = jnp.max(peaks, axis=0)
        row_total = jnp.sum(totals * jnp.exp(peaks - row_peak[None]), axis=0)
        stats = jnp.stack([row_peak, row_total, jnp.sum(stacked[:, 2], axis=0)])
    weight_float = stats[2].reshape(-1)
    log_sum = (stats[0] + jnp.log(stats[1])).reshape(-1)

    responsibility = (weight_float[:, None] * jnp.exp(scores - log_sum[:, None])).astype(jnp.bfloat16)
    grouped_resp = responsibility.reshape(n_groups, -1, own_count)
    grouped_rows = unit_rows.reshape(n_groups, -1, width)
    partial_value = lax.dot_general(
        grouped_resp, grouped_rows, (((1,), (1,)), ((0,), (0,))), preferred_element_type=jnp.float32
    ).astype(jnp.bfloat16)
    centroid_sums = jnp.sum(partial_value.astype(jnp.float32), axis=0)
    weight_mass = jnp.sum(grouped_resp.astype(jnp.float32), axis=1).astype(jnp.bfloat16)
    own_mass = jnp.sum(weight_mass.astype(jnp.float32), axis=0)

    moved = own_cents.astype(jnp.float32) + centroid_sums / (own_mass + 1.0)[:, None]
    renormed = normalize(moved).astype(jnp.bfloat16)

    own_log_sum = log_sum.reshape(block_shape)[own_index[:-1]]
    objective = weights.astype(jnp.float32) * own_log_sum / sharpness
    return (centroid_sums, renormed, objective)


def solution(mesh):
    in_specs = (
        P(("groups", "cent", "dp", "sub"), None),
        P(("groups", "cent", "dp", "sub")),
        P(("groups", "cent"), None),
        P(),
    )
    out_specs = (
        P(("groups", "cent", "dp", "sub"), None),
        P(("groups", "cent", "dp", "sub"), None),
        P(("groups", "cent", "dp", "sub")),
    )
    return jax.shard_map(shards, mesh=mesh, in_specs=in_specs, out_specs=out_specs, check_vma=False)
```

```python
import jax
import jax.numpy as jnp
from jax import lax
from jax.sharding import PartitionSpec as P

STAGES = ("cent", "dp", "sub")
SHIFT_MAX = 4


def normalize(values):
    floats = values.astype(jnp.float32)
    return floats * lax.rsqrt(jnp.sum(floats * floats, axis=-1, keepdims=True) + 1e-06)


def relative(name):
    return lax.axis_size(name) <= SHIFT_MAX


def gather_stage(value, name):
    size = lax.axis_size(name)
    if relative(name):
        parts = [value] + [
            lax.ppermute(value, name, [(j, (j + q) % size) for j in range(size)]) for q in range(1, size)
        ]
        return jnp.stack(parts)
    return lax.all_gather(value, name, axis=0)


def own_block(name):
    return 0 if relative(name) else lax.axis_index(name)


def merge_stats(stats, names, block_axis):
    for name in names:
        size = lax.axis_size(name)
        stacked = gather_stage(stats, name)
        if relative(name):
            stacked = jnp.stack([jnp.roll(stacked[q], q, axis=block_axis[name]) for q in range(size)])
        peaks, totals = stacked[:, 0], stacked[:, 1]
        row_peak = jnp.max(peaks, axis=0)
        row_total = jnp.sum(totals * jnp.exp(peaks - row_peak[None]), axis=0)
        stats = jnp.stack([row_peak, row_total, jnp.max(stacked[:, 2], axis=0)])
    return stats


def shards(embeddings, weights, centroids, inverse_temp):
    sharpness = inverse_temp[0]
    row_dev, width = embeddings.shape
    sizes = {name: lax.axis_size(name) for name in STAGES}
    n_groups = sizes["dp"] * sizes["sub"]
    panel = centroids.shape[0]
    own_count = panel // n_groups
    n_rows = row_dev * sizes["cent"] * n_groups
    full_panel = n_rows * panel * 4 <= (16 << 20)

    blocks = gather_stage(embeddings, "cent").reshape(-1, width)
    cent_rows = blocks.shape[0]
    weight_block = jnp.pad(weights.astype(jnp.bfloat16)[None, :], ((0, 15), (0, width - row_dev)))
    payload = jnp.concatenate([blocks, weight_block], axis=0)
    for name in STAGES[1:]:
        payload = gather_stage(payload, name)
    unit_rows = normalize(payload[:, :, :cent_rows].reshape(-1, width)).astype(jnp.bfloat16)
    cent_weights = payload[:, :, cent_rows, :row_dev].astype(jnp.float32)

    offset = lax.axis_index(("dp", "sub")) * own_count
    if full_panel:
        panel_cents = lax.optimization_barrier(normalize(centroids).astype(jnp.bfloat16))
        own_cents = lax.dynamic_slice_in_dim(panel_cents, offset, own_count, 0)
        score_cents = panel_cents
    else:
        own_cents = normalize(lax.dynamic_slice_in_dim(centroids, offset, own_count, 0)).astype(jnp.bfloat16)
        own_cents = lax.optimization_barrier(own_cents)
        score_cents = own_cents

    scores = (
        lax.dot_general(
            unit_rows, score_cents, (((1,), (1,)), ((), ())), preferred_element_type=jnp.float32
        )
        * sharpness
    )
    block_shape = (sizes["sub"], sizes["dp"], sizes["cent"], row_dev)
    local_peak = jnp.max(scores, axis=1)
    local_total = jnp.sum(jnp.exp(scores - local_peak[:, None]), axis=1)
    if full_panel:
        scores = lax.dynamic_slice_in_dim(scores, offset, own_count, 1)

    own_cent = own_block("cent")
    known_weights = lax.dynamic_update_slice(
        jnp.zeros(block_shape, jnp.float32), cent_weights[:, :, None], (0, 0, own_cent, 0)
    )
    stats = jnp.stack([local_peak.reshape(block_shape), local_total.reshape(block_shape), known_weights])
    stats = merge_stats(stats, STAGES[:1] if full_panel else STAGES, {"sub": 1, "dp": 2, "cent": 3})
    weight_float = stats[2].reshape(-1)
    log_sum = (stats[0] + jnp.log(stats[1])).reshape(-1)

    responsibility = (weight_float[:, None] * jnp.exp(scores - log_sum[:, None])).astype(jnp.bfloat16)
    grouped_resp = responsibility.reshape(n_groups, -1, own_count)
    grouped_rows = unit_rows.reshape(n_groups, -1, width)
    partial_value = lax.dot_general(
        grouped_resp, grouped_rows, (((1,), (1,)), ((0,), (0,))), preferred_element_type=jnp.float32
    ).astype(jnp.bfloat16)
    centroid_sums = jnp.sum(partial_value.astype(jnp.float32), axis=0)
    weight_mass = jnp.sum(grouped_resp.astype(jnp.float32), axis=1).astype(jnp.bfloat16)
    own_mass = jnp.sum(weight_mass.astype(jnp.float32), axis=0)

    moved = own_cents.astype(jnp.float32) + centroid_sums / (own_mass + 1.0)[:, None]
    renormed = normalize(moved).astype(jnp.bfloat16)

    own_log_sum = log_sum.reshape(block_shape)[own_block("sub"), own_block("dp"), own_cent]
    objective = weights.astype(jnp.float32) * own_log_sum / sharpness
    return (centroid_sums, renormed, objective)


def solution(mesh):
    in_specs = (
        P(("groups", "cent", "dp", "sub"), None),
        P(("groups", "cent", "dp", "sub")),
        P(("groups", "cent"), None),
        P(),
    )
    out_specs = (
        P(("groups", "cent", "dp", "sub"), None),
        P(("groups", "cent", "dp", "sub"), None),
        P(("groups", "cent", "dp", "sub")),
    )
    return jax.shard_map(shards, mesh=mesh, in_specs=in_specs, out_specs=out_specs, check_vma=False)
```

```python
import jax
import jax.numpy as jnp
from jax import lax
from jax.experimental import pallas as pl
from jax.sharding import PartitionSpec as P

STAGES = ("cent", "dp", "sub")
SHIFT_MAX = 4
GROUP_ROWS = 128


def normalize(values):
    floats = values.astype(jnp.float32)
    return floats * lax.rsqrt(jnp.sum(floats * floats, axis=-1, keepdims=True) + 1e-06)


def relative(name):
    return lax.axis_size(name) <= SHIFT_MAX


def gather_stage(value, name):
    size = lax.axis_size(name)
    if relative(name):
        parts = [value] + [
            lax.ppermute(value, name, [(j, (j + q) % size) for j in range(size)]) for q in range(1, size)
        ]
        return jnp.stack(parts)
    return lax.all_gather(value, name, axis=0)


def own_block(name):
    return 0 if relative(name) else lax.axis_index(name)


def update_kernel(scores_ref, log_sum_ref, weight_ref, rows_ref, cents_ref, sums_ref, renormed_ref):
    n_groups = rows_ref.shape[0] // GROUP_ROWS
    responsibility = (weight_ref[...] * jnp.exp(scores_ref[...] - log_sum_ref[...])).astype(jnp.bfloat16)
    sums = jnp.zeros(sums_ref.shape, jnp.float32)
    mass = jnp.zeros((sums_ref.shape[0], 1), jnp.float32)
    for group in range(n_groups):
        part = responsibility[:, group * GROUP_ROWS:(group + 1) * GROUP_ROWS]
        partial_value = jnp.dot(
            part, rows_ref[group * GROUP_ROWS:(group + 1) * GROUP_ROWS, :], preferred_element_type=jnp.float32
        )
        sums = sums + partial_value.astype(jnp.bfloat16).astype(jnp.float32)
        group_mass = jnp.sum(part.astype(jnp.float32), axis=1, keepdims=True)
        mass = mass + group_mass.astype(jnp.bfloat16).astype(jnp.float32)
    sums_ref[...] = sums
    moved = cents_ref[...].astype(jnp.float32) + sums / (mass + 1.0)
    renormed_ref[...] = (moved * lax.rsqrt(jnp.sum(moved * moved, axis=1, keepdims=True) + 1e-06)).astype(
        jnp.bfloat16
    )


def shards(embeddings, weights, centroids, inverse_temp):
    sharpness = inverse_temp[0]
    row_dev, width = embeddings.shape
    sizes = {name: lax.axis_size(name) for name in STAGES}
    n_groups = sizes["dp"] * sizes["sub"]
    own_count = centroids.shape[0] // n_groups

    blocks = embeddings
    for name in STAGES:
        blocks = gather_stage(blocks, name)
    unit_rows = normalize(blocks.reshape(-1, width)).astype(jnp.bfloat16)

    offset = lax.axis_index(("dp", "sub")) * own_count
    own_cents = normalize(lax.dynamic_slice_in_dim(centroids, offset, own_count, 0)).astype(jnp.bfloat16)
    own_cents = lax.optimization_barrier(own_cents)

    scores = (
        lax.dot_general(
            own_cents, unit_rows, (((1,), (1,)), ((), ())), preferred_element_type=jnp.float32
        )
        * sharpness
    )
    block_shape = (sizes["sub"], sizes["dp"], sizes["cent"], row_dev)
    local_peak = jnp.max(scores, axis=0)
    local_total = jnp.sum(jnp.exp(scores - local_peak[None, :]), axis=0)

    own_index = (own_block("sub"), own_block("dp"), own_block("cent"), 0)
    known_weights = lax.dynamic_update_slice(
        jnp.zeros(block_shape, jnp.float32), weights.astype(jnp.float32)[None, None, None], own_index
    )
    stats = jnp.stack([local_peak.reshape(block_shape), local_total.reshape(block_shape), known_weights])
    block_axis = {"sub": 1, "dp": 2, "cent": 3}
    for name in STAGES:
        stacked = gather_stage(stats, name)
        if relative(name):
            stacked = jnp.stack(
                [jnp.roll(stacked[q], q, axis=block_axis[name]) for q in range(sizes[name])]
            )
        peaks, totals = stacked[:, 0], stacked[:, 1]
        row_peak = jnp.max(peaks, axis=0)
        row_total = jnp.sum(totals * jnp.exp(peaks - row_peak[None]), axis=0)
        stats = jnp.stack([row_peak, row_total, jnp.sum(stacked[:, 2], axis=0)])
    weight_float = stats[2].reshape(-1)
    log_sum = (stats[0] + jnp.log(stats[1])).reshape(-1)

    n_rows = unit_rows.shape[0]
    if n_rows == n_groups * GROUP_ROWS and n_rows * (own_count + width) * 4 <= (8 << 20):
        centroid_sums, renormed = pl.pallas_call(
            update_kernel,
            out_shape=(
                jax.ShapeDtypeStruct((own_count, width), jnp.float32),
                jax.ShapeDtypeStruct((own_count, width), jnp.bfloat16),
            ),
        )(scores, log_sum[None, :], weight_float[None, :], unit_rows, own_cents)
    else:
        responsibility = (weight_float[None, :] * jnp.exp(scores - log_sum[None, :])).astype(jnp.bfloat16)
        grouped_resp = responsibility.reshape(own_count, n_groups, -1)
        grouped_rows = unit_rows.reshape(n_groups, -1, width)
        partial_value = lax.dot_general(
            grouped_resp, grouped_rows, (((2,), (1,)), ((1,), (0,))), preferred_element_type=jnp.float32
        ).astype(jnp.bfloat16)
        centroid_sums = jnp.sum(partial_value.astype(jnp.float32), axis=0)
        weight_mass = jnp.sum(grouped_resp.astype(jnp.float32), axis=2).astype(jnp.bfloat16)
        own_mass = jnp.sum(weight_mass.astype(jnp.float32), axis=1)
        moved = own_cents.astype(jnp.float32) + centroid_sums / (own_mass + 1.0)[:, None]
        renormed = normalize(moved).astype(jnp.bfloat16)

    own_log_sum = log_sum.reshape(block_shape)[own_index[:3]]
    objective = weights.astype(jnp.float32) * own_log_sum / sharpness
    return (centroid_sums, renormed, objective)


def solution(mesh):
    in_specs = (
        P(("groups", "cent", "dp", "sub"), None),
        P(("groups", "cent", "dp", "sub")),
        P(("groups", "cent"), None),
        P(),
    )
    out_specs = (
        P(("groups", "cent", "dp", "sub"), None),
        P(("groups", "cent", "dp", "sub"), None),
        P(("groups", "cent", "dp", "sub")),
    )
    return jax.shard_map(shards, mesh=mesh, in_specs=in_specs, out_specs=out_specs, check_vma=False)
```

```python
import jax
import jax.numpy as jnp
from jax import lax
from jax.sharding import PartitionSpec as P

STAGES = ("cent", "dp", "sub")
SHIFT_MAX = 4


def normalize(values):
    floats = values.astype(jnp.float32)
    return floats * lax.rsqrt(jnp.sum(floats * floats, axis=-1, keepdims=True) + 1e-06)


def relative(name):
    return lax.axis_size(name) <= SHIFT_MAX


def gather_stage(value, name):
    size = lax.axis_size(name)
    if relative(name):
        parts = [value] + [
            lax.ppermute(value, name, [(j, (j + q) % size) for j in range(size)]) for q in range(1, size)
        ]
        return jnp.stack(parts)
    return lax.all_gather(value, name, axis=0)


def own_block(name):
    return 0 if relative(name) else lax.axis_index(name)


def merge_stats(stats, names, block_axis):
    for name in names:
        size = lax.axis_size(name)
        stacked = gather_stage(stats, name)
        if relative(name):
            stacked = jnp.stack([jnp.roll(stacked[q], q, axis=block_axis[name]) for q in range(size)])
        peaks, totals = stacked[:, 0], stacked[:, 1]
        row_peak = jnp.max(peaks, axis=0)
        row_total = jnp.sum(totals * jnp.exp(peaks - row_peak[None]), axis=0)
        stats = jnp.stack([row_peak, row_total, jnp.max(stacked[:, 2], axis=0)])
    return stats


def shards(embeddings, weights, centroids, inverse_temp):
    sharpness = inverse_temp[0]
    row_dev, width = embeddings.shape
    sizes = {name: lax.axis_size(name) for name in STAGES}
    n_groups = sizes["dp"] * sizes["sub"]
    panel = centroids.shape[0]
    own_count = panel // n_groups
    n_rows = row_dev * sizes["cent"] * n_groups
    dp_columns = n_rows * own_count * sizes["dp"] * 4 <= (16 << 20)

    blocks = gather_stage(embeddings, "cent").reshape(-1, width)
    cent_rows = blocks.shape[0]
    weight_block = jnp.pad(weights.astype(jnp.bfloat16)[None, :], ((0, 15), (0, width - row_dev)))
    payload = jnp.concatenate([blocks, weight_block], axis=0)
    for name in STAGES[1:]:
        payload = gather_stage(payload, name)
    unit_rows = normalize(payload[:, :, :cent_rows].reshape(-1, width)).astype(jnp.bfloat16)
    cent_weights = payload[:, :, cent_rows, :row_dev].astype(jnp.float32)

    offset = lax.axis_index(("dp", "sub")) * own_count
    if dp_columns:
        dp_index, sub_index = lax.axis_index("dp"), lax.axis_index("sub")
        slices = [
            lax.dynamic_slice_in_dim(
                centroids, ((dp_index + q) % sizes["dp"] * sizes["sub"] + sub_index) * own_count, own_count, 0
            )
            for q in range(sizes["dp"])
        ]
        score_cents = lax.optimization_barrier(normalize(jnp.concatenate(slices, axis=0)).astype(jnp.bfloat16))
        own_cents = score_cents[:own_count]
    else:
        own_cents = normalize(lax.dynamic_slice_in_dim(centroids, offset, own_count, 0)).astype(jnp.bfloat16)
        own_cents = lax.optimization_barrier(own_cents)
        score_cents = own_cents

    scores = (
        lax.dot_general(
            unit_rows, score_cents, (((1,), (1,)), ((), ())), preferred_element_type=jnp.float32
        )
        * sharpness
    )
    block_shape = (sizes["sub"], sizes["dp"], sizes["cent"], row_dev)
    local_peak = jnp.max(scores, axis=1)
    local_total = jnp.sum(jnp.exp(scores - local_peak[:, None]), axis=1)
    if dp_columns:
        scores = scores[:, :own_count]

    own_cent = own_block("cent")
    known_weights = lax.dynamic_update_slice(
        jnp.zeros(block_shape, jnp.float32), cent_weights[:, :, None], (0, 0, own_cent, 0)
    )
    stats = jnp.stack([local_peak.reshape(block_shape), local_total.reshape(block_shape), known_weights])
    stats = merge_stats(stats, ("cent", "sub") if dp_columns else STAGES, {"sub": 1, "dp": 2, "cent": 3})
    weight_float = stats[2].reshape(-1)
    log_sum = (stats[0] + jnp.log(stats[1])).reshape(-1)

    responsibility = (weight_float[:, None] * jnp.exp(scores - log_sum[:, None])).astype(jnp.bfloat16)
    grouped_resp = responsibility.reshape(n_groups, -1, own_count)
    grouped_rows = unit_rows.reshape(n_groups, -1, width)
    partial_value = lax.dot_general(
        grouped_resp, grouped_rows, (((1,), (1,)), ((0,), (0,))), preferred_element_type=jnp.float32
    ).astype(jnp.bfloat16)
    centroid_sums = jnp.sum(partial_value.astype(jnp.float32), axis=0)
    weight_mass = jnp.sum(grouped_resp.astype(jnp.float32), axis=1).astype(jnp.bfloat16)
    own_mass = jnp.sum(weight_mass.astype(jnp.float32), axis=0)

    moved = own_cents.astype(jnp.float32) + centroid_sums / (own_mass + 1.0)[:, None]
    renormed = normalize(moved).astype(jnp.bfloat16)

    own_log_sum = log_sum.reshape(block_shape)[own_block("sub"), own_block("dp"), own_cent]
    objective = weights.astype(jnp.float32) * own_log_sum / sharpness
    return (centroid_sums, renormed, objective)


def solution(mesh):
    in_specs = (
        P(("groups", "cent", "dp", "sub"), None),
        P(("groups", "cent", "dp", "sub")),
        P(("groups", "cent"), None),
        P(),
    )
    out_specs = (
        P(("groups", "cent", "dp", "sub"), None),
        P(("groups", "cent", "dp", "sub"), None),
        P(("groups", "cent", "dp", "sub")),
    )
    return jax.shard_map(shards, mesh=mesh, in_specs=in_specs, out_specs=out_specs, check_vma=False)
```

```python
import jax
import jax.numpy as jnp
from jax import lax
from jax.sharding import PartitionSpec as P

STAGES = ("cent", "dp", "sub")
SHIFT_MAX = 4


def normalize(values):
    floats = values.astype(jnp.float32)
    return floats * lax.rsqrt(jnp.sum(floats * floats, axis=-1, keepdims=True) + 1e-06)


def relative(name):
    return lax.axis_size(name) <= SHIFT_MAX


def gather_stage(value, name):
    size = lax.axis_size(name)
    if relative(name):
        parts = [value] + [
            lax.ppermute(value, name, [(j, (j + q) % size) for j in range(size)]) for q in range(1, size)
        ]
        return jnp.stack(parts)
    return lax.all_gather(value, name, axis=0)


def own_block(name):
    return 0 if relative(name) else lax.axis_index(name)


def merge_stats(stats, names, block_axis):
    for name in names:
        size = lax.axis_size(name)
        stacked = gather_stage(stats, name)
        if relative(name):
            stacked = jnp.stack([jnp.roll(stacked[q], q, axis=block_axis[name]) for q in range(size)])
        peaks, totals = stacked[:, 0], stacked[:, 1]
        row_peak = jnp.max(peaks, axis=0)
        row_total = jnp.sum(totals * jnp.exp(peaks - row_peak[None]), axis=0)
        stats = jnp.stack([row_peak, row_total, jnp.max(stacked[:, 2], axis=0)])
    return stats


def shards(embeddings, weights, centroids, inverse_temp):
    sharpness = inverse_temp[0]
    row_dev, width = embeddings.shape
    sizes = {name: lax.axis_size(name) for name in STAGES}
    n_groups = sizes["dp"] * sizes["sub"]
    panel = centroids.shape[0]
    own_count = panel // n_groups
    n_rows = row_dev * sizes["cent"] * n_groups
    dp_columns = n_rows * own_count * sizes["dp"] * 4 <= (16 << 20)

    blocks = gather_stage(embeddings, "cent").reshape(-1, width)
    cent_rows = blocks.shape[0]
    weight_block = jnp.pad(weights.astype(jnp.bfloat16)[None, :], ((0, 15), (0, width - row_dev)))
    payload = jnp.concatenate([blocks, weight_block], axis=0)
    for name in STAGES[1:]:
        payload = gather_stage(payload, name)
    unit_rows = normalize(payload[:, :, :cent_rows].reshape(-1, width)).astype(jnp.bfloat16)
    cent_weights = payload[:, :, cent_rows, :row_dev].astype(jnp.float32)

    offset = lax.axis_index(("dp", "sub")) * own_count
    if dp_columns:
        dp_index, sub_index = lax.axis_index("dp"), lax.axis_index("sub")
        score_cents = [
            lax.optimization_barrier(
                normalize(
                    lax.dynamic_slice_in_dim(
                        centroids, ((dp_index + q) % sizes["dp"] * sizes["sub"] + sub_index) * own_count, own_count, 0
                    )
                ).astype(jnp.bfloat16)
            )
            for q in range(sizes["dp"])
        ]
    else:
        own_cents = normalize(lax.dynamic_slice_in_dim(centroids, offset, own_count, 0)).astype(jnp.bfloat16)
        score_cents = [lax.optimization_barrier(own_cents)]
    own_cents = score_cents[0]

    score_blocks = [
        lax.dot_general(unit_rows, cents, (((1,), (1,)), ((), ())), preferred_element_type=jnp.float32)
        * sharpness
        for cents in score_cents
    ]
    scores = score_blocks[0]
    block_shape = (sizes["sub"], sizes["dp"], sizes["cent"], row_dev)
    local_peak = score_blocks[0].max(axis=1)
    for block in score_blocks[1:]:
        local_peak = jnp.maximum(local_peak, block.max(axis=1))
    local_total = sum(jnp.sum(jnp.exp(block - local_peak[:, None]), axis=1) for block in score_blocks)

    own_cent = own_block("cent")
    known_weights = lax.dynamic_update_slice(
        jnp.zeros(block_shape, jnp.float32), cent_weights[:, :, None], (0, 0, own_cent, 0)
    )
    stats = jnp.stack([local_peak.reshape(block_shape), local_total.reshape(block_shape), known_weights])
    stats = merge_stats(stats, ("cent", "sub") if dp_columns else STAGES, {"sub": 1, "dp": 2, "cent": 3})
    weight_float = stats[2].reshape(-1)
    log_sum = (stats[0] + jnp.log(stats[1])).reshape(-1)

    responsibility = (weight_float[:, None] * jnp.exp(scores - log_sum[:, None])).astype(jnp.bfloat16)
    grouped_resp = responsibility.reshape(n_groups, -1, own_count)
    grouped_rows = unit_rows.reshape(n_groups, -1, width)
    partial_value = lax.dot_general(
        grouped_resp, grouped_rows, (((1,), (1,)), ((0,), (0,))), preferred_element_type=jnp.float32
    ).astype(jnp.bfloat16)
    centroid_sums = jnp.sum(partial_value.astype(jnp.float32), axis=0)
    weight_mass = jnp.sum(grouped_resp.astype(jnp.float32), axis=1).astype(jnp.bfloat16)
    own_mass = jnp.sum(weight_mass.astype(jnp.float32), axis=0)

    moved = own_cents.astype(jnp.float32) + centroid_sums / (own_mass + 1.0)[:, None]
    renormed = normalize(moved).astype(jnp.bfloat16)

    own_log_sum = log_sum.reshape(block_shape)[own_block("sub"), own_block("dp"), own_cent]
    objective = weights.astype(jnp.float32) * own_log_sum / sharpness
    return (centroid_sums, renormed, objective)


def solution(mesh):
    in_specs = (
        P(("groups", "cent", "dp", "sub"), None),
        P(("groups", "cent", "dp", "sub")),
        P(("groups", "cent"), None),
        P(),
    )
    out_specs = (
        P(("groups", "cent", "dp", "sub"), None),
        P(("groups", "cent", "dp", "sub"), None),
        P(("groups", "cent", "dp", "sub")),
    )
    return jax.shard_map(shards, mesh=mesh, in_specs=in_specs, out_specs=out_specs, check_vma=False)
```

```python
import jax
import jax.numpy as jnp
from jax import lax
from jax.sharding import PartitionSpec as P

STAGES = ("cent", "dp", "sub")
SHIFT_MAX = 4


def normalize(values):
    floats = values.astype(jnp.float32)
    return floats * lax.rsqrt(jnp.sum(floats * floats, axis=-1, keepdims=True) + 1e-06)


def relative(name):
    return lax.axis_size(name) <= SHIFT_MAX


def gather_stage(value, name):
    size = lax.axis_size(name)
    if relative(name):
        parts = [value] + [
            lax.ppermute(value, name, [(j, (j + q) % size) for j in range(size)]) for q in range(1, size)
        ]
        return jnp.stack(parts)
    return lax.all_gather(value, name, axis=0)


def own_block(name):
    return 0 if relative(name) else lax.axis_index(name)


def merge_stats(stats, names, block_axis):
    for name in names:
        size = lax.axis_size(name)
        stacked = gather_stage(stats, name)
        if relative(name):
            stacked = jnp.stack([jnp.roll(stacked[q], q, axis=block_axis[name]) for q in range(size)])
        peaks, totals = stacked[:, 0], stacked[:, 1]
        row_peak = jnp.max(peaks, axis=0)
        row_total = jnp.sum(totals * jnp.exp(peaks - row_peak[None]), axis=0)
        stats = jnp.stack([row_peak, row_total, jnp.max(stacked[:, 2], axis=0)])
    return stats


def shards(embeddings, weights, centroids, inverse_temp):
    sharpness = inverse_temp[0]
    row_dev, width = embeddings.shape
    sizes = {name: lax.axis_size(name) for name in STAGES}
    n_groups = sizes["dp"] * sizes["sub"]
    panel = centroids.shape[0]
    own_count = panel // n_groups
    n_rows = row_dev * sizes["cent"] * n_groups
    dp_columns = n_rows * own_count * sizes["dp"] * 4 <= (16 << 20)

    blocks = gather_stage(embeddings, "cent").reshape(-1, width)
    cent_rows = blocks.shape[0]
    weight_block = jnp.pad(weights.astype(jnp.bfloat16)[None, :], ((0, 15), (0, width - row_dev)))
    payload = jnp.concatenate([blocks, weight_block], axis=0)
    for name in STAGES[1:]:
        payload = gather_stage(payload, name)
    halves = [
        normalize(payload[half, :, :cent_rows].reshape(-1, width)).astype(jnp.bfloat16) for half in range(sizes["sub"])
    ]
    cent_weights = payload[:, :, cent_rows, :row_dev].astype(jnp.float32)

    offset = lax.axis_index(("dp", "sub")) * own_count
    if dp_columns:
        dp_index, sub_index = lax.axis_index("dp"), lax.axis_index("sub")
        score_cents = [
            lax.optimization_barrier(
                normalize(
                    lax.dynamic_slice_in_dim(
                        centroids, ((dp_index + q) % sizes["dp"] * sizes["sub"] + sub_index) * own_count, own_count, 0
                    )
                ).astype(jnp.bfloat16)
            )
            for q in range(sizes["dp"])
        ]
    else:
        own_cents = normalize(lax.dynamic_slice_in_dim(centroids, offset, own_count, 0)).astype(jnp.bfloat16)
        score_cents = [lax.optimization_barrier(own_cents)]
    own_cents = score_cents[0]

    score_blocks = [
        [
            lax.dot_general(rows, cents, (((1,), (1,)), ((), ())), preferred_element_type=jnp.float32) * sharpness
            for cents in score_cents
        ]
        for rows in halves
    ]
    block_shape = (sizes["sub"], sizes["dp"], sizes["cent"], row_dev)
    peaks, totals = [], []
    for blocks_of_half in score_blocks:
        half_peak = blocks_of_half[0].max(axis=1)
        for block in blocks_of_half[1:]:
            half_peak = jnp.maximum(half_peak, block.max(axis=1))
        peaks.append(half_peak)
        totals.append(sum(jnp.sum(jnp.exp(block - half_peak[:, None]), axis=1) for block in blocks_of_half))
    local_peak = jnp.concatenate(peaks)
    local_total = jnp.concatenate(totals)

    own_cent = own_block("cent")
    known_weights = lax.dynamic_update_slice(
        jnp.zeros(block_shape, jnp.float32), cent_weights[:, :, None], (0, 0, own_cent, 0)
    )
    stats = jnp.stack([local_peak.reshape(block_shape), local_total.reshape(block_shape), known_weights])
    stats = merge_stats(stats, ("cent", "sub") if dp_columns else STAGES, {"sub": 1, "dp": 2, "cent": 3})
    weight_float = stats[2].reshape(-1)
    log_sum = (stats[0] + jnp.log(stats[1])).reshape(-1)

    half_log_sum = log_sum.reshape(sizes["sub"], -1)
    half_weight = weight_float.reshape(sizes["sub"], -1)
    centroid_sums = jnp.zeros((own_count, width), jnp.float32)
    own_mass = jnp.zeros((own_count,), jnp.float32)
    for half, rows in enumerate(halves):
        responsibility = (
            half_weight[half][:, None] * jnp.exp(score_blocks[half][0] - half_log_sum[half][:, None])
        ).astype(jnp.bfloat16)
        grouped_resp = responsibility.reshape(sizes["dp"], -1, own_count)
        grouped_rows = rows.reshape(sizes["dp"], -1, width)
        partial_value = lax.dot_general(
            grouped_resp, grouped_rows, (((1,), (1,)), ((0,), (0,))), preferred_element_type=jnp.float32
        ).astype(jnp.bfloat16)
        centroid_sums = centroid_sums + jnp.sum(partial_value.astype(jnp.float32), axis=0)
        weight_mass = jnp.sum(grouped_resp.astype(jnp.float32), axis=1).astype(jnp.bfloat16)
        own_mass = own_mass + jnp.sum(weight_mass.astype(jnp.float32), axis=0)

    moved = own_cents.astype(jnp.float32) + centroid_sums / (own_mass + 1.0)[:, None]
    renormed = normalize(moved).astype(jnp.bfloat16)

    own_log_sum = log_sum.reshape(block_shape)[own_block("sub"), own_block("dp"), own_cent]
    objective = weights.astype(jnp.float32) * own_log_sum / sharpness
    return (centroid_sums, renormed, objective)


def solution(mesh):
    in_specs = (
        P(("groups", "cent", "dp", "sub"), None),
        P(("groups", "cent", "dp", "sub")),
        P(("groups", "cent"), None),
        P(),
    )
    out_specs = (
        P(("groups", "cent", "dp", "sub"), None),
        P(("groups", "cent", "dp", "sub"), None),
        P(("groups", "cent", "dp", "sub")),
    )
    return jax.shard_map(shards, mesh=mesh, in_specs=in_specs, out_specs=out_specs, check_vma=False)
```

```python
import jax
import numpy as np
import jax.numpy as jnp
from jax import lax
from jax.sharding import PartitionSpec as P

STAGES = ("cent", "dp", "sub")
SHIFT_MAX = 4


def normalize(values):
    floats = values.astype(jnp.float32)
    return floats * lax.rsqrt(jnp.sum(floats * floats, axis=-1, keepdims=True) + 1e-06)


def relative(name):
    return lax.axis_size(name) <= SHIFT_MAX


def partner(index, step, size):
    if size & (size - 1):
        return (index + step) % size
    return index ^ step


def gather_stage(value, name):
    size = lax.axis_size(name)
    if relative(name):
        parts = [value] + [
            lax.ppermute(value, name, [(j, partner(j, q, size)) for j in range(size)]) for q in range(1, size)
        ]
        return jnp.stack(parts)
    return lax.all_gather(value, name, axis=0)


def align(received, step, size, axis):
    if size & (size - 1):
        return jnp.roll(received, step, axis=axis)
    return jnp.take(received, np.array([p ^ step for p in range(size)]), axis=axis)


def own_block(name):
    return 0 if relative(name) else lax.axis_index(name)


def merge_stats(stats, names, block_axis):
    for name in names:
        size = lax.axis_size(name)
        stacked = gather_stage(stats, name)
        if relative(name):
            stacked = jnp.stack([align(stacked[q], q, size, block_axis[name]) for q in range(size)])
        peaks, totals = stacked[:, 0], stacked[:, 1]
        row_peak = jnp.max(peaks, axis=0)
        row_total = jnp.sum(totals * jnp.exp(peaks - row_peak[None]), axis=0)
        stats = jnp.stack([row_peak, row_total, jnp.max(stacked[:, 2], axis=0)])
    return stats


def shards(embeddings, weights, centroids, inverse_temp):
    sharpness = inverse_temp[0]
    row_dev, width = embeddings.shape
    sizes = {name: lax.axis_size(name) for name in STAGES}
    n_groups = sizes["dp"] * sizes["sub"]
    panel = centroids.shape[0]
    own_count = panel // n_groups
    n_rows = row_dev * sizes["cent"] * n_groups
    dp_columns = n_rows * own_count * sizes["dp"] * 4 <= (16 << 20)

    blocks = gather_stage(embeddings, "cent").reshape(-1, width)
    cent_rows = blocks.shape[0]
    weight_block = jnp.pad(weights.astype(jnp.bfloat16)[None, :], ((0, 15), (0, width - row_dev)))
    payload = jnp.concatenate([blocks, weight_block], axis=0)
    for name in STAGES[1:]:
        payload = gather_stage(payload, name)
    halves = [
        normalize(payload[half, :, :cent_rows].reshape(-1, width)).astype(jnp.bfloat16) for half in range(sizes["sub"])
    ]
    cent_weights = payload[:, :, cent_rows, :row_dev].astype(jnp.float32)

    offset = lax.axis_index(("dp", "sub")) * own_count
    if dp_columns:
        dp_index, sub_index = lax.axis_index("dp"), lax.axis_index("sub")
        score_cents = [
            lax.optimization_barrier(
                normalize(
                    lax.dynamic_slice_in_dim(
                        centroids, ((dp_index + q) % sizes["dp"] * sizes["sub"] + sub_index) * own_count, own_count, 0
                    )
                ).astype(jnp.bfloat16)
            )
            for q in range(sizes["dp"])
        ]
    else:
        own_cents = normalize(lax.dynamic_slice_in_dim(centroids, offset, own_count, 0)).astype(jnp.bfloat16)
        score_cents = [lax.optimization_barrier(own_cents)]
    own_cents = score_cents[0]

    score_blocks = [
        [
            lax.dot_general(rows, cents, (((1,), (1,)), ((), ())), preferred_element_type=jnp.float32) * sharpness
            for cents in score_cents
        ]
        for rows in halves
    ]
    block_shape = (sizes["sub"], sizes["dp"], sizes["cent"], row_dev)
    peaks, totals = [], []
    for blocks_of_half in score_blocks:
        half_peak = blocks_of_half[0].max(axis=1)
        for block in blocks_of_half[1:]:
            half_peak = jnp.maximum(half_peak, block.max(axis=1))
        peaks.append(half_peak)
        totals.append(sum(jnp.sum(jnp.exp(block - half_peak[:, None]), axis=1) for block in blocks_of_half))
    local_peak = jnp.concatenate(peaks)
    local_total = jnp.concatenate(totals)

    own_cent = own_block("cent")
    known_weights = lax.dynamic_update_slice(
        jnp.zeros(block_shape, jnp.float32), cent_weights[:, :, None], (0, 0, own_cent, 0)
    )
    stats = jnp.stack([local_peak.reshape(block_shape), local_total.reshape(block_shape), known_weights])
    stats = merge_stats(stats, ("cent", "sub") if dp_columns else STAGES, {"sub": 1, "dp": 2, "cent": 3})
    weight_float = stats[2].reshape(-1)
    log_sum = (stats[0] + jnp.log(stats[1])).reshape(-1)

    half_log_sum = log_sum.reshape(sizes["sub"], -1)
    half_weight = weight_float.reshape(sizes["sub"], -1)
    centroid_sums = jnp.zeros((own_count, width), jnp.float32)
    own_mass = jnp.zeros((own_count,), jnp.float32)
    for half, rows in enumerate(halves):
        responsibility = (
            half_weight[half][:, None] * jnp.exp(score_blocks[half][0] - half_log_sum[half][:, None])
        ).astype(jnp.bfloat16)
        grouped_resp = responsibility.reshape(sizes["dp"], -1, own_count)
        grouped_rows = rows.reshape(sizes["dp"], -1, width)
        partial_value = lax.dot_general(
            grouped_resp, grouped_rows, (((1,), (1,)), ((0,), (0,))), preferred_element_type=jnp.float32
        ).astype(jnp.bfloat16)
        centroid_sums = centroid_sums + jnp.sum(partial_value.astype(jnp.float32), axis=0)
        weight_mass = jnp.sum(grouped_resp.astype(jnp.float32), axis=1).astype(jnp.bfloat16)
        own_mass = own_mass + jnp.sum(weight_mass.astype(jnp.float32), axis=0)

    moved = own_cents.astype(jnp.float32) + centroid_sums / (own_mass + 1.0)[:, None]
    renormed = normalize(moved).astype(jnp.bfloat16)

    own_rows = (own_block("sub"), own_block("dp"), own_cent)
    objective = (weight_float.reshape(block_shape)[own_rows] * log_sum.reshape(block_shape)[own_rows]) / sharpness
    return (centroid_sums, renormed, objective)


def solution(mesh):
    in_specs = (
        P(("groups", "cent", "dp", "sub"), None),
        P(("groups", "cent", "dp", "sub")),
        P(("groups", "cent"), None),
        P(),
    )
    out_specs = (
        P(("groups", "cent", "dp", "sub"), None),
        P(("groups", "cent", "dp", "sub"), None),
        P(("groups", "cent", "dp", "sub")),
    )
    return jax.shard_map(shards, mesh=mesh, in_specs=in_specs, out_specs=out_specs, check_vma=False)
```

```python
import jax
import jax.numpy as jnp
from jax import lax
from jax.sharding import PartitionSpec as P

STAGES = ("cent", "dp", "sub")
SHIFT_MAX = 4


def normalize(values):
    floats = values.astype(jnp.float32)
    return floats * lax.rsqrt(jnp.sum(floats * floats, axis=-1, keepdims=True) + 1e-06)


def relative(name):
    return lax.axis_size(name) <= SHIFT_MAX


def gather_stage(value, name):
    size = lax.axis_size(name)
    if relative(name):
        parts = [value] + [
            lax.ppermute(value, name, [(j, (j + q) % size) for j in range(size)]) for q in range(1, size)
        ]
        return jnp.stack(parts)
    return lax.all_gather(value, name, axis=0)


def own_block(name):
    return 0 if relative(name) else lax.axis_index(name)


def merge_stats(stats, names, block_axis):
    for name in names:
        size = lax.axis_size(name)
        stacked = gather_stage(stats, name)
        if relative(name):
            stacked = jnp.stack([jnp.roll(stacked[q], q, axis=block_axis[name]) for q in range(size)])
        peaks, totals = stacked[:, 0], stacked[:, 1]
        row_peak = jnp.max(peaks, axis=0)
        row_total = jnp.sum(totals * jnp.exp(peaks - row_peak[None]), axis=0)
        stats = jnp.stack([row_peak, row_total, jnp.max(stacked[:, 2], axis=0)])
    return stats


def shards(embeddings, weights, centroids, inverse_temp):
    sharpness = inverse_temp[0]
    row_dev, width = embeddings.shape
    sizes = {name: lax.axis_size(name) for name in STAGES}
    n_groups = sizes["dp"] * sizes["sub"]
    panel = centroids.shape[0]
    own_count = panel // n_groups
    n_rows = row_dev * sizes["cent"] * n_groups
    dp_columns = n_rows * own_count * sizes["dp"] * 4 <= (16 << 20)

    blocks = gather_stage(embeddings, "cent").reshape(-1, width)
    cent_rows = blocks.shape[0]
    weight_block = jnp.pad(weights.astype(jnp.bfloat16)[None, :], ((0, 15), (0, width - row_dev)))
    payload = jnp.concatenate([blocks, weight_block], axis=0)
    for name in STAGES[1:]:
        payload = gather_stage(payload, name)
    halves = [
        normalize(payload[half, :, :cent_rows].reshape(-1, width)).astype(jnp.bfloat16) for half in range(sizes["sub"])
    ]
    cent_weights = payload[:, :, cent_rows, :row_dev].astype(jnp.float32)

    offset = lax.axis_index(("dp", "sub")) * own_count
    if dp_columns:
        dp_index, sub_index = lax.axis_index("dp"), lax.axis_index("sub")
        score_cents = [
            lax.optimization_barrier(
                normalize(
                    lax.dynamic_slice_in_dim(
                        centroids, ((dp_index + q) % sizes["dp"] * sizes["sub"] + sub_index) * own_count, own_count, 0
                    )
                ).astype(jnp.bfloat16)
            )
            for q in range(sizes["dp"])
        ]
    else:
        own_cents = normalize(lax.dynamic_slice_in_dim(centroids, offset, own_count, 0)).astype(jnp.bfloat16)
        score_cents = [lax.optimization_barrier(own_cents)]
    own_cents = score_cents[0]

    score_blocks = [
        [
            lax.dot_general(rows, cents, (((1,), (1,)), ((), ())), preferred_element_type=jnp.float32) * sharpness
            for cents in score_cents
        ]
        for rows in halves
    ]
    block_shape = (sizes["sub"], sizes["dp"], sizes["cent"], row_dev)
    peaks, totals = [], []
    for blocks_of_half in score_blocks:
        half_peak = blocks_of_half[0].max(axis=1)
        for block in blocks_of_half[1:]:
            half_peak = jnp.maximum(half_peak, block.max(axis=1))
        peaks.append(half_peak)
        totals.append(sum(jnp.sum(jnp.exp(block - half_peak[:, None]), axis=1) for block in blocks_of_half))
    local_peak = jnp.concatenate(peaks)
    local_total = jnp.concatenate(totals)

    own_cent = own_block("cent")
    known_weights = lax.dynamic_update_slice(
        jnp.zeros(block_shape, jnp.float32), cent_weights[:, :, None], (0, 0, own_cent, 0)
    )
    stats = jnp.stack([local_peak.reshape(block_shape), local_total.reshape(block_shape), known_weights])
    stats = merge_stats(stats, ("cent", "sub") if dp_columns else STAGES, {"sub": 1, "dp": 2, "cent": 3})
    weight_float = stats[2].reshape(-1)
    log_sum = (stats[0] + jnp.log(stats[1])).reshape(-1)

    half_log_sum = log_sum.reshape(sizes["sub"], -1)
    half_weight = weight_float.reshape(sizes["sub"], -1)
    centroid_sums = jnp.zeros((own_count, width), jnp.float32)
    own_mass = jnp.zeros((own_count,), jnp.float32)
    for half, rows in enumerate(halves):
        responsibility = (
            half_weight[half][:, None] * jnp.exp(score_blocks[half][0] - half_log_sum[half][:, None])
        ).astype(jnp.bfloat16)
        grouped_resp = responsibility.reshape(sizes["dp"], -1, own_count)
        grouped_rows = rows.reshape(sizes["dp"], -1, width)
        partial_value = lax.dot_general(
            grouped_resp, grouped_rows, (((1,), (1,)), ((0,), (0,))), preferred_element_type=jnp.float32
        ).astype(jnp.bfloat16)
        centroid_sums = centroid_sums + jnp.sum(partial_value.astype(jnp.float32), axis=0)
        weight_mass = jnp.sum(grouped_resp.astype(jnp.float32), axis=1).astype(jnp.bfloat16)
        own_mass = own_mass + jnp.sum(weight_mass.astype(jnp.float32), axis=0)

    moved = own_cents.astype(jnp.float32) + centroid_sums / (own_mass + 1.0)[:, None]
    renormed = normalize(moved).astype(jnp.bfloat16)

    own_rows = (own_block("sub"), own_block("dp"), own_cent)
    objective = (weight_float.reshape(block_shape)[own_rows] * log_sum.reshape(block_shape)[own_rows]) / sharpness
    return (centroid_sums, renormed, objective)


def solution(mesh):
    in_specs = (
        P(("groups", "cent", "dp", "sub"), None),
        P(("groups", "cent", "dp", "sub")),
        P(("groups", "cent"), None),
        P(),
    )
    out_specs = (
        P(("groups", "cent", "dp", "sub"), None),
        P(("groups", "cent", "dp", "sub"), None),
        P(("groups", "cent", "dp", "sub")),
    )
    return jax.shard_map(shards, mesh=mesh, in_specs=in_specs, out_specs=out_specs, check_vma=False)
```

```python
import jax
import jax.numpy as jnp
from jax import lax
from jax.sharding import PartitionSpec as P

STAGES = ("cent", "dp", "sub")
SHIFT_MAX = 4


def normalize(values):
    floats = values.astype(jnp.float32)
    return floats * lax.rsqrt(jnp.sum(floats * floats, axis=-1, keepdims=True) + 1e-06)


def relative(name):
    return lax.axis_size(name) <= SHIFT_MAX


def gather_stage(value, name):
    size = lax.axis_size(name)
    if relative(name):
        parts = [value] + [
            lax.ppermute(value, name, [(j, (j + q) % size) for j in range(size)]) for q in range(1, size)
        ]
        return jnp.stack(parts)
    return lax.all_gather(value, name, axis=0)


def own_block(name):
    return 0 if relative(name) else lax.axis_index(name)


def merge_stats(stats, names, block_axis):
    for name in names:
        size = lax.axis_size(name)
        stacked = gather_stage(stats, name)
        if relative(name):
            stacked = jnp.stack([jnp.roll(stacked[q], q, axis=block_axis[name]) for q in range(size)])
        peaks, totals = stacked[:, 0], stacked[:, 1]
        row_peak = jnp.max(peaks, axis=0)
        row_total = jnp.sum(totals * jnp.exp(peaks - row_peak[None]), axis=0)
        stats = jnp.stack([row_peak, row_total, jnp.max(stacked[:, 2], axis=0)])
    return stats


def shards(embeddings, weights, centroids, inverse_temp):
    sharpness = inverse_temp[0]
    row_dev, width = embeddings.shape
    sizes = {name: lax.axis_size(name) for name in STAGES}
    n_groups = sizes["dp"] * sizes["sub"]
    panel = centroids.shape[0]
    own_count = panel // n_groups
    n_rows = row_dev * sizes["cent"] * n_groups
    dp_columns = n_rows * own_count * sizes["dp"] * 4 <= (16 << 20)

    blocks = gather_stage(embeddings, "cent").reshape(-1, width)
    cent_rows = blocks.shape[0]
    weight_block = jnp.pad(weights.astype(jnp.bfloat16)[None, :], ((0, 15), (0, width - row_dev)))
    payload = jnp.concatenate([blocks, weight_block], axis=0)
    if sizes["dp"] == 2 and sizes["sub"] == 2:
        from_dp = gather_stage(payload, "dp")[1]
        from_sub = gather_stage(payload, "sub")[1]
        from_diagonal = gather_stage(from_dp, "sub")[1]
        pieces = [payload, from_dp, from_sub, from_diagonal]
    else:
        for name in STAGES[1:]:
            payload = gather_stage(payload, name)
        pieces = [payload[half] for half in range(sizes["sub"])]
    chunks = [
        normalize(piece[..., :cent_rows, :].reshape(-1, width)).astype(jnp.bfloat16) for piece in pieces
    ]
    cent_weights = jnp.stack([piece[..., cent_rows, :row_dev] for piece in pieces]).astype(jnp.float32)
    cent_weights = cent_weights.reshape(sizes["sub"], sizes["dp"], row_dev)

    offset = lax.axis_index(("dp", "sub")) * own_count
    if dp_columns:
        dp_index, sub_index = lax.axis_index("dp"), lax.axis_index("sub")
        score_cents = [
            lax.optimization_barrier(
                normalize(
                    lax.dynamic_slice_in_dim(
                        centroids, ((dp_index + q) % sizes["dp"] * sizes["sub"] + sub_index) * own_count, own_count, 0
                    )
                ).astype(jnp.bfloat16)
            )
            for q in range(sizes["dp"])
        ]
    else:
        own_cents = normalize(lax.dynamic_slice_in_dim(centroids, offset, own_count, 0)).astype(jnp.bfloat16)
        score_cents = [lax.optimization_barrier(own_cents)]
    own_cents = score_cents[0]

    score_blocks = [
        [
            lax.dot_general(rows, cents, (((1,), (1,)), ((), ())), preferred_element_type=jnp.float32) * sharpness
            for cents in score_cents
        ]
        for rows in chunks
    ]
    block_shape = (sizes["sub"], sizes["dp"], sizes["cent"], row_dev)
    peaks, totals = [], []
    for blocks_of_half in score_blocks:
        half_peak = blocks_of_half[0].max(axis=1)
        for block in blocks_of_half[1:]:
            half_peak = jnp.maximum(half_peak, block.max(axis=1))
        peaks.append(half_peak)
        totals.append(sum(jnp.sum(jnp.exp(block - half_peak[:, None]), axis=1) for block in blocks_of_half))
    local_peak = jnp.concatenate(peaks)
    local_total = jnp.concatenate(totals)

    own_cent = own_block("cent")
    known_weights = lax.dynamic_update_slice(
        jnp.zeros(block_shape, jnp.float32), cent_weights[:, :, None], (0, 0, own_cent, 0)
    )
    stats = jnp.stack([local_peak.reshape(block_shape), local_total.reshape(block_shape), known_weights])
    stats = merge_stats(stats, ("cent", "sub") if dp_columns else STAGES, {"sub": 1, "dp": 2, "cent": 3})
    weight_float = stats[2].reshape(-1)
    log_sum = (stats[0] + jnp.log(stats[1])).reshape(-1)

    own_scores = jnp.stack([blocks_of_chunk[0] for blocks_of_chunk in score_blocks]).reshape(n_groups, -1, own_count)
    grouped_rows = jnp.stack(chunks).reshape(n_groups, -1, width)
    grouped_resp = (
        weight_float.reshape(n_groups, -1, 1) * jnp.exp(own_scores - log_sum.reshape(n_groups, -1, 1))
    ).astype(jnp.bfloat16)
    partial_value = lax.dot_general(
        grouped_resp, grouped_rows, (((1,), (1,)), ((0,), (0,))), preferred_element_type=jnp.float32
    ).astype(jnp.bfloat16)
    centroid_sums = jnp.sum(partial_value.astype(jnp.float32), axis=0)
    weight_mass = jnp.sum(grouped_resp.astype(jnp.float32), axis=1).astype(jnp.bfloat16)
    own_mass = jnp.sum(weight_mass.astype(jnp.float32), axis=0)

    moved = own_cents.astype(jnp.float32) + centroid_sums / (own_mass + 1.0)[:, None]
    renormed = normalize(moved).astype(jnp.bfloat16)

    own_rows = (own_block("sub"), own_block("dp"), own_cent)
    objective = (weight_float.reshape(block_shape)[own_rows] * log_sum.reshape(block_shape)[own_rows]) / sharpness
    return (centroid_sums, renormed, objective)


def solution(mesh):
    in_specs = (
        P(("groups", "cent", "dp", "sub"), None),
        P(("groups", "cent", "dp", "sub")),
        P(("groups", "cent"), None),
        P(),
    )
    out_specs = (
        P(("groups", "cent", "dp", "sub"), None),
        P(("groups", "cent", "dp", "sub"), None),
        P(("groups", "cent", "dp", "sub")),
    )
    return jax.shard_map(shards, mesh=mesh, in_specs=in_specs, out_specs=out_specs, check_vma=False)
```

```python
import jax
import jax.numpy as jnp
from jax import lax
from jax.sharding import PartitionSpec as P

STAGES = ("cent", "dp", "sub")
SHIFT_MAX = 4


def normalize(values):
    floats = values.astype(jnp.float32)
    return floats * lax.rsqrt(jnp.sum(floats * floats, axis=-1, keepdims=True) + 1e-06)


def relative(name):
    return lax.axis_size(name) <= SHIFT_MAX


def gather_stage(value, name):
    size = lax.axis_size(name)
    if relative(name):
        parts = [value] + [
            lax.ppermute(value, name, [(j, (j + q) % size) for j in range(size)]) for q in range(1, size)
        ]
        return jnp.stack(parts)
    return lax.all_gather(value, name, axis=0)


def own_block(name):
    return 0 if relative(name) else lax.axis_index(name)


def merge_stats(stats, names, block_axis):
    for name in names:
        size = lax.axis_size(name)
        stacked = gather_stage(stats, name)
        if relative(name):
            stacked = jnp.stack([jnp.roll(stacked[q], q, axis=block_axis[name]) for q in range(size)])
        peaks, totals = stacked[:, 0], stacked[:, 1]
        row_peak = jnp.max(peaks, axis=0)
        row_total = jnp.sum(totals * jnp.exp(peaks - row_peak[None]), axis=0)
        stats = jnp.stack([row_peak, row_total, jnp.max(stacked[:, 2], axis=0)])
    return stats


def shards(embeddings, weights, centroids, inverse_temp):
    sharpness = inverse_temp[0]
    row_dev, width = embeddings.shape
    sizes = {name: lax.axis_size(name) for name in STAGES}
    n_groups = sizes["dp"] * sizes["sub"]
    panel = centroids.shape[0]
    own_count = panel // n_groups
    n_rows = row_dev * sizes["cent"] * n_groups
    dp_columns = n_rows * own_count * sizes["dp"] * 4 <= (16 << 20)

    blocks = gather_stage(embeddings, "cent").reshape(-1, width)
    cent_rows = blocks.shape[0]
    weight_block = jnp.pad(weights.astype(jnp.bfloat16)[None, :], ((0, 15), (0, width - row_dev)))
    payload = jnp.concatenate([blocks, weight_block], axis=0)
    for name in STAGES[1:]:
        payload = gather_stage(payload, name)
    halves = [
        normalize(payload[half, :, :cent_rows].reshape(-1, width)).astype(jnp.bfloat16) for half in range(sizes["sub"])
    ]
    cent_weights = payload[:, :, cent_rows, :row_dev].astype(jnp.float32)

    offset = lax.axis_index(("dp", "sub")) * own_count
    if dp_columns:
        dp_index, sub_index = lax.axis_index("dp"), lax.axis_index("sub")
        score_cents = [
            lax.optimization_barrier(
                normalize(
                    lax.dynamic_slice_in_dim(
                        centroids, ((dp_index + q) % sizes["dp"] * sizes["sub"] + sub_index) * own_count, own_count, 0
                    )
                ).astype(jnp.bfloat16)
            )
            for q in range(sizes["dp"])
        ]
    else:
        own_cents = normalize(lax.dynamic_slice_in_dim(centroids, offset, own_count, 0)).astype(jnp.bfloat16)
        score_cents = [lax.optimization_barrier(own_cents)]
    own_cents = score_cents[0]

    score_blocks = [
        [
            lax.dot_general(rows, cents, (((1,), (1,)), ((), ())), preferred_element_type=jnp.float32) * sharpness
            for cents in score_cents
        ]
        for rows in halves
    ]
    block_shape = (sizes["sub"], sizes["dp"], sizes["cent"], row_dev)
    peaks, totals = [], []
    for blocks_of_half in score_blocks:
        half_peak = blocks_of_half[0].max(axis=1)
        for block in blocks_of_half[1:]:
            half_peak = jnp.maximum(half_peak, block.max(axis=1))
        peaks.append(half_peak)
        totals.append(sum(jnp.sum(jnp.exp(block - half_peak[:, None]), axis=1) for block in blocks_of_half))
    local_peak = jnp.concatenate(peaks)
    local_total = jnp.concatenate(totals)

    own_cent = own_block("cent")
    known_weights = lax.dynamic_update_slice(
        jnp.zeros(block_shape, jnp.float32), cent_weights[:, :, None], (0, 0, own_cent, 0)
    )
    stats = jnp.stack([local_peak.reshape(block_shape), local_total.reshape(block_shape), known_weights])
    stats = merge_stats(stats, ("cent", "sub") if dp_columns else STAGES, {"sub": 1, "dp": 2, "cent": 3})
    weight_float = stats[2].reshape(-1)
    log_sum = (stats[0] + jnp.log(stats[1])).reshape(-1)

    if sum(rows.size for rows in halves) * 2 <= (4 << 20):
        own_scores = jnp.stack([blocks_of_half[0] for blocks_of_half in score_blocks]).reshape(n_groups, -1, own_count)
        grouped_rows = jnp.stack(halves).reshape(n_groups, -1, width)
        grouped_resp = (
            weight_float.reshape(n_groups, -1, 1) * jnp.exp(own_scores - log_sum.reshape(n_groups, -1, 1))
        ).astype(jnp.bfloat16)
        partial_value = lax.dot_general(
            grouped_resp, grouped_rows, (((1,), (1,)), ((0,), (0,))), preferred_element_type=jnp.float32
        ).astype(jnp.bfloat16)
        centroid_sums = jnp.sum(partial_value.astype(jnp.float32), axis=0)
        weight_mass = jnp.sum(grouped_resp.astype(jnp.float32), axis=1).astype(jnp.bfloat16)
        own_mass = jnp.sum(weight_mass.astype(jnp.float32), axis=0)
    else:
        half_log_sum = log_sum.reshape(sizes["sub"], -1)
        half_weight = weight_float.reshape(sizes["sub"], -1)
        centroid_sums = jnp.zeros((own_count, width), jnp.float32)
        own_mass = jnp.zeros((own_count,), jnp.float32)
        for half, rows in enumerate(halves):
            responsibility = (
                half_weight[half][:, None] * jnp.exp(score_blocks[half][0] - half_log_sum[half][:, None])
            ).astype(jnp.bfloat16)
            grouped_resp = responsibility.reshape(sizes["dp"], -1, own_count)
            grouped_rows = rows.reshape(sizes["dp"], -1, width)
            partial_value = lax.dot_general(
                grouped_resp, grouped_rows, (((1,), (1,)), ((0,), (0,))), preferred_element_type=jnp.float32
            ).astype(jnp.bfloat16)
            centroid_sums = centroid_sums + jnp.sum(partial_value.astype(jnp.float32), axis=0)
            weight_mass = jnp.sum(grouped_resp.astype(jnp.float32), axis=1).astype(jnp.bfloat16)
            own_mass = own_mass + jnp.sum(weight_mass.astype(jnp.float32), axis=0)

    moved = own_cents.astype(jnp.float32) + centroid_sums / (own_mass + 1.0)[:, None]
    renormed = normalize(moved).astype(jnp.bfloat16)

    own_log_sum = log_sum.reshape(block_shape)[own_block("sub"), own_block("dp"), own_cent]
    objective = weights.astype(jnp.float32) * own_log_sum / sharpness
    return (centroid_sums, renormed, objective)


def solution(mesh):
    in_specs = (
        P(("groups", "cent", "dp", "sub"), None),
        P(("groups", "cent", "dp", "sub")),
        P(("groups", "cent"), None),
        P(),
    )
    out_specs = (
        P(("groups", "cent", "dp", "sub"), None),
        P(("groups", "cent", "dp", "sub"), None),
        P(("groups", "cent", "dp", "sub")),
    )
    return jax.shard_map(shards, mesh=mesh, in_specs=in_specs, out_specs=out_specs, check_vma=False)
```

```python
import jax
import jax.numpy as jnp
from jax import lax
from jax.sharding import PartitionSpec as P

STAGES = ("cent", "dp", "sub")
SHIFT_MAX = 4


def normalize(values):
    floats = values.astype(jnp.float32)
    return floats * lax.rsqrt(jnp.sum(floats * floats, axis=-1, keepdims=True) + 1e-06)


def relative(name):
    return lax.axis_size(name) <= SHIFT_MAX


def gather_stage(value, name):
    size = lax.axis_size(name)
    if relative(name):
        parts = [value] + [
            lax.ppermute(value, name, [(j, (j + q) % size) for j in range(size)]) for q in range(1, size)
        ]
        return jnp.stack(parts)
    return lax.all_gather(value, name, axis=0)


def own_block(name):
    return 0 if relative(name) else lax.axis_index(name)


def merge_stats(stats, names, block_axis):
    for name in names:
        size = lax.axis_size(name)
        stacked = gather_stage(stats, name)
        if relative(name):
            stacked = jnp.stack([jnp.roll(stacked[q], q, axis=block_axis[name]) for q in range(size)])
        peaks, totals = stacked[:, 0], stacked[:, 1]
        row_peak = jnp.max(peaks, axis=0)
        row_total = jnp.sum(totals * jnp.exp(peaks - row_peak[None]), axis=0)
        stats = jnp.stack([row_peak, row_total, jnp.max(stacked[:, 2], axis=0)])
    return stats


def shards(embeddings, weights, centroids, inverse_temp):
    sharpness = inverse_temp[0]
    row_dev, width = embeddings.shape
    sizes = {name: lax.axis_size(name) for name in STAGES}
    n_groups = sizes["dp"] * sizes["sub"]
    panel = centroids.shape[0]
    own_count = panel // n_groups
    n_rows = row_dev * sizes["cent"] * n_groups
    dp_columns = n_rows * own_count * sizes["dp"] * 4 <= (16 << 20)

    blocks = gather_stage(embeddings, "cent").reshape(-1, width)
    cent_rows = blocks.shape[0]
    weight_block = jnp.pad(weights.astype(jnp.bfloat16)[None, :], ((0, 15), (0, width - row_dev)))
    payload = jnp.concatenate([blocks, weight_block], axis=0)
    for name in STAGES[1:]:
        payload = gather_stage(payload, name)
    halves = [
        normalize(payload[half, :, :cent_rows].reshape(-1, width)).astype(jnp.bfloat16) for half in range(sizes["sub"])
    ]
    cent_weights = payload[:, :, cent_rows, :row_dev].astype(jnp.float32)

    offset = lax.axis_index(("dp", "sub")) * own_count
    if dp_columns:
        dp_index, sub_index = lax.axis_index("dp"), lax.axis_index("sub")
        slices = [
            lax.dynamic_slice_in_dim(
                centroids, ((dp_index + q) % sizes["dp"] * sizes["sub"] + sub_index) * own_count, own_count, 0
            )
            for q in range(sizes["dp"])
        ]
        score_cents = lax.optimization_barrier(normalize(jnp.concatenate(slices, axis=0)).astype(jnp.bfloat16))
    else:
        own_cents = normalize(lax.dynamic_slice_in_dim(centroids, offset, own_count, 0)).astype(jnp.bfloat16)
        score_cents = lax.optimization_barrier(own_cents)
    own_cents = score_cents[:own_count]

    score_blocks = [
        lax.dot_general(rows, score_cents, (((1,), (1,)), ((), ())), preferred_element_type=jnp.float32) * sharpness
        for rows in halves
    ]
    block_shape = (sizes["sub"], sizes["dp"], sizes["cent"], row_dev)
    peaks, totals = [], []
    for block in score_blocks:
        half_peak = block.max(axis=1)
        peaks.append(half_peak)
        totals.append(jnp.sum(jnp.exp(block - half_peak[:, None]), axis=1))
    local_peak = jnp.concatenate(peaks)
    local_total = jnp.concatenate(totals)

    own_cent = own_block("cent")
    known_weights = lax.dynamic_update_slice(
        jnp.zeros(block_shape, jnp.float32), cent_weights[:, :, None], (0, 0, own_cent, 0)
    )
    stats = jnp.stack([local_peak.reshape(block_shape), local_total.reshape(block_shape), known_weights])
    stats = merge_stats(stats, ("cent", "sub") if dp_columns else STAGES, {"sub": 1, "dp": 2, "cent": 3})
    weight_float = stats[2].reshape(-1)
    log_sum = (stats[0] + jnp.log(stats[1])).reshape(-1)

    half_log_sum = log_sum.reshape(sizes["sub"], -1)
    half_weight = weight_float.reshape(sizes["sub"], -1)
    centroid_sums = jnp.zeros((own_count, width), jnp.float32)
    own_mass = jnp.zeros((own_count,), jnp.float32)
    for half, rows in enumerate(halves):
        responsibility = (
            half_weight[half][:, None] * jnp.exp(score_blocks[half][:, :own_count] - half_log_sum[half][:, None])
        ).astype(jnp.bfloat16)
        grouped_resp = responsibility.reshape(sizes["dp"], -1, own_count)
        grouped_rows = rows.reshape(sizes["dp"], -1, width)
        partial_value = lax.dot_general(
            grouped_resp, grouped_rows, (((1,), (1,)), ((0,), (0,))), preferred_element_type=jnp.float32
        ).astype(jnp.bfloat16)
        centroid_sums = centroid_sums + jnp.sum(partial_value.astype(jnp.float32), axis=0)
        weight_mass = jnp.sum(grouped_resp.astype(jnp.float32), axis=1).astype(jnp.bfloat16)
        own_mass = own_mass + jnp.sum(weight_mass.astype(jnp.float32), axis=0)

    moved = own_cents.astype(jnp.float32) + centroid_sums / (own_mass + 1.0)[:, None]
    renormed = normalize(moved).astype(jnp.bfloat16)

    own_log_sum = log_sum.reshape(block_shape)[own_block("sub"), own_block("dp"), own_cent]
    objective = weights.astype(jnp.float32) * own_log_sum / sharpness
    return (centroid_sums, renormed, objective)


def solution(mesh):
    in_specs = (
        P(("groups", "cent", "dp", "sub"), None),
        P(("groups", "cent", "dp", "sub")),
        P(("groups", "cent"), None),
        P(),
    )
    out_specs = (
        P(("groups", "cent", "dp", "sub"), None),
        P(("groups", "cent", "dp", "sub"), None),
        P(("groups", "cent", "dp", "sub")),
    )
    return jax.shard_map(shards, mesh=mesh, in_specs=in_specs, out_specs=out_specs, check_vma=False)
```

```python
import jax
import jax.numpy as jnp
from jax import lax
from jax.sharding import PartitionSpec as P

STAGES = ("cent", "dp", "sub")
SHIFT_MAX = 4


def normalize(values):
    floats = values.astype(jnp.float32)
    return floats * lax.rsqrt(jnp.sum(floats * floats, axis=-1, keepdims=True) + 1e-06)


def relative(name):
    return lax.axis_size(name) <= SHIFT_MAX


def gather_stage(value, name):
    size = lax.axis_size(name)
    if relative(name):
        parts = [value] + [
            lax.ppermute(value, name, [(j, (j + q) % size) for j in range(size)]) for q in range(1, size)
        ]
        return jnp.stack(parts)
    return lax.all_gather(value, name, axis=0)


def own_block(name):
    return 0 if relative(name) else lax.axis_index(name)


def merge_stats(stats, names, block_axis):
    for name in names:
        size = lax.axis_size(name)
        stacked = gather_stage(stats, name)
        if relative(name):
            stacked = jnp.stack([jnp.roll(stacked[q], q, axis=block_axis[name]) for q in range(size)])
        peaks, totals = stacked[:, 0], stacked[:, 1]
        row_peak = jnp.max(peaks, axis=0)
        row_total = jnp.sum(totals * jnp.exp(peaks - row_peak[None]), axis=0)
        stats = jnp.stack([row_peak, row_total, jnp.max(stacked[:, 2], axis=0)])
    return stats


def shards(embeddings, weights, centroids, inverse_temp):
    sharpness = inverse_temp[0]
    row_dev, width = embeddings.shape
    sizes = {name: lax.axis_size(name) for name in STAGES}
    n_groups = sizes["dp"] * sizes["sub"]
    panel = centroids.shape[0]
    own_count = panel // n_groups
    n_rows = row_dev * sizes["cent"] * n_groups
    dp_columns = n_rows * own_count * sizes["dp"] * 4 <= (16 << 20)

    blocks = gather_stage(embeddings, "cent").reshape(-1, width)
    cent_rows = blocks.shape[0]
    weight_block = jnp.pad(weights.astype(jnp.bfloat16)[None, :], ((0, 15), (0, width - row_dev)))
    payload = jnp.concatenate([blocks, weight_block], axis=0)
    for name in STAGES[1:]:
        payload = gather_stage(payload, name)
    halves = [
        normalize(payload[half, :, :cent_rows].reshape(-1, width)).astype(jnp.bfloat16) for half in range(sizes["sub"])
    ]
    cent_weights = payload[:, :, cent_rows, :row_dev].astype(jnp.float32)

    offset = lax.axis_index(("dp", "sub")) * own_count
    if dp_columns:
        dp_index, sub_index = lax.axis_index("dp"), lax.axis_index("sub")
        score_cents = [
            lax.optimization_barrier(
                normalize(
                    lax.dynamic_slice_in_dim(
                        centroids, ((dp_index + q) % sizes["dp"] * sizes["sub"] + sub_index) * own_count, own_count, 0
                    )
                ).astype(jnp.bfloat16)
            )
            for q in range(sizes["dp"])
        ]
    else:
        own_cents = normalize(lax.dynamic_slice_in_dim(centroids, offset, own_count, 0)).astype(jnp.bfloat16)
        score_cents = [lax.optimization_barrier(own_cents)]
    own_cents = score_cents[0]

    score_blocks = [
        [
            lax.dot_general(rows, cents, (((1,), (1,)), ((), ())), preferred_element_type=jnp.float32) * sharpness
            for cents in score_cents
        ]
        for rows in halves
    ]
    block_shape = (sizes["sub"], sizes["dp"], sizes["cent"], row_dev)
    peaks, totals = [], []
    for blocks_of_half in score_blocks:
        half_peak = blocks_of_half[0].max(axis=1)
        for block in blocks_of_half[1:]:
            half_peak = jnp.maximum(half_peak, block.max(axis=1))
        peaks.append(half_peak)
        totals.append(sum(jnp.sum(jnp.exp(block - half_peak[:, None]), axis=1) for block in blocks_of_half))
    local_peak = jnp.concatenate(peaks)
    local_total = jnp.concatenate(totals)

    own_cent = own_block("cent")
    known_weights = lax.dynamic_update_slice(
        jnp.zeros(block_shape, jnp.float32), cent_weights[:, :, None], (0, 0, own_cent, 0)
    )
    stats = jnp.stack([local_peak.reshape(block_shape), local_total.reshape(block_shape), known_weights])
    stats = merge_stats(stats, ("cent", "sub") if dp_columns else STAGES, {"sub": 1, "dp": 2, "cent": 3})
    weight_float = stats[2].reshape(-1)
    log_sum = (stats[0] + jnp.log(stats[1])).reshape(-1)

    half_log_sum = log_sum.reshape(sizes["sub"], -1)
    half_weight = weight_float.reshape(sizes["sub"], -1)
    centroid_sums = jnp.zeros((own_count, width), jnp.float32)
    own_mass = jnp.zeros((own_count,), jnp.float32)
    for half, rows in enumerate(halves):
        responsibility = (
            half_weight[half][:, None] * jnp.exp(score_blocks[half][0] - half_log_sum[half][:, None])
        ).astype(jnp.bfloat16)
        grouped_resp = responsibility.reshape(sizes["dp"], -1, own_count)
        grouped_rows = rows.reshape(sizes["dp"], -1, width)
        partial_value = lax.dot_general(
            grouped_resp, grouped_rows, (((1,), (1,)), ((0,), (0,))), preferred_element_type=jnp.float32
        ).astype(jnp.bfloat16)
        centroid_sums = centroid_sums + jnp.sum(partial_value.astype(jnp.float32), axis=0)
        weight_mass = jnp.sum(grouped_resp.astype(jnp.float32), axis=1).astype(jnp.bfloat16)
        own_mass = own_mass + jnp.sum(weight_mass.astype(jnp.float32), axis=0)

    moved = lax.optimization_barrier(own_cents.astype(jnp.float32) + centroid_sums / (own_mass + 1.0)[:, None])
    renormed = normalize(moved).astype(jnp.bfloat16)

    own_log_sum = log_sum.reshape(block_shape)[own_block("sub"), own_block("dp"), own_cent]
    objective = weights.astype(jnp.float32) * own_log_sum / sharpness
    return (centroid_sums, renormed, objective)


def solution(mesh):
    in_specs = (
        P(("groups", "cent", "dp", "sub"), None),
        P(("groups", "cent", "dp", "sub")),
        P(("groups", "cent"), None),
        P(),
    )
    out_specs = (
        P(("groups", "cent", "dp", "sub"), None),
        P(("groups", "cent", "dp", "sub"), None),
        P(("groups", "cent", "dp", "sub")),
    )
    return jax.shard_map(shards, mesh=mesh, in_specs=in_specs, out_specs=out_specs, check_vma=False)
```

```python
import jax
import jax.numpy as jnp
from jax import lax
from jax.sharding import PartitionSpec as P

STAGES = ("cent", "dp", "sub")
SHIFT_MAX = 4


def normalize(values):
    floats = values.astype(jnp.float32)
    return floats * lax.rsqrt(jnp.sum(floats * floats, axis=-1, keepdims=True) + 1e-06)


def relative(name):
    return lax.axis_size(name) <= SHIFT_MAX


def partner(index, step, size):
    if size & (size - 1):
        return (index + step) % size
    return index ^ step


def gather_stage(value, name):
    size = lax.axis_size(name)
    if relative(name):
        parts = [value] + [
            lax.ppermute(value, name, [(j, partner(j, q, size)) for j in range(size)]) for q in range(1, size)
        ]
        return jnp.stack(parts)
    return lax.all_gather(value, name, axis=0)


def align(received, step, size, axis):
    if size & (size - 1):
        return jnp.roll(received, step, axis=axis)
    shape = received.shape
    bit = 1
    while bit < size:
        if step & bit:
            split = shape[:axis] + (size // (2 * bit), 2, bit) + shape[axis + 1:]
            received = jnp.flip(received.reshape(split), axis=axis + 1).reshape(shape)
        bit *= 2
    return received


def own_block(name):
    return 0 if relative(name) else lax.axis_index(name)


def merge_stats(stats, names, block_axis):
    for name in names:
        size = lax.axis_size(name)
        stacked = gather_stage(stats, name)
        if relative(name):
            stacked = jnp.stack([align(stacked[q], q, size, block_axis[name]) for q in range(size)])
        peaks, totals = stacked[:, 0], stacked[:, 1]
        row_peak = jnp.max(peaks, axis=0)
        row_total = jnp.sum(totals * jnp.exp(peaks - row_peak[None]), axis=0)
        stats = jnp.stack([row_peak, row_total, jnp.max(stacked[:, 2], axis=0)])
    return stats


def shards(embeddings, weights, centroids, inverse_temp):
    sharpness = inverse_temp[0]
    row_dev, width = embeddings.shape
    sizes = {name: lax.axis_size(name) for name in STAGES}
    n_groups = sizes["dp"] * sizes["sub"]
    panel = centroids.shape[0]
    own_count = panel // n_groups
    n_rows = row_dev * sizes["cent"] * n_groups
    dp_columns = n_rows * own_count * sizes["dp"] * 4 <= (16 << 20)

    blocks = gather_stage(embeddings, "cent").reshape(-1, width)
    cent_rows = blocks.shape[0]
    weight_block = jnp.pad(weights.astype(jnp.bfloat16)[None, :], ((0, 15), (0, width - row_dev)))
    payload = jnp.concatenate([blocks, weight_block], axis=0)
    for name in STAGES[1:]:
        payload = gather_stage(payload, name)
    halves = [
        normalize(payload[half, :, :cent_rows].reshape(-1, width)).astype(jnp.bfloat16) for half in range(sizes["sub"])
    ]
    cent_weights = payload[:, :, cent_rows, :row_dev].astype(jnp.float32)

    offset = lax.axis_index(("dp", "sub")) * own_count
    if dp_columns:
        dp_index, sub_index = lax.axis_index("dp"), lax.axis_index("sub")
        score_cents = [
            lax.optimization_barrier(
                normalize(
                    lax.dynamic_slice_in_dim(
                        centroids, ((dp_index + q) % sizes["dp"] * sizes["sub"] + sub_index) * own_count, own_count, 0
                    )
                ).astype(jnp.bfloat16)
            )
            for q in range(sizes["dp"])
        ]
    else:
        own_cents = normalize(lax.dynamic_slice_in_dim(centroids, offset, own_count, 0)).astype(jnp.bfloat16)
        score_cents = [lax.optimization_barrier(own_cents)]
    own_cents = score_cents[0]

    score_blocks = [
        [
            lax.dot_general(rows, cents, (((1,), (1,)), ((), ())), preferred_element_type=jnp.float32) * sharpness
            for cents in score_cents
        ]
        for rows in halves
    ]
    block_shape = (sizes["sub"], sizes["dp"], sizes["cent"], row_dev)
    peaks, totals = [], []
    for blocks_of_half in score_blocks:
        half_peak = blocks_of_half[0].max(axis=1)
        for block in blocks_of_half[1:]:
            half_peak = jnp.maximum(half_peak, block.max(axis=1))
        peaks.append(half_peak)
        totals.append(sum(jnp.sum(jnp.exp(block - half_peak[:, None]), axis=1) for block in blocks_of_half))
    local_peak = jnp.concatenate(peaks)
    local_total = jnp.concatenate(totals)

    own_cent = own_block("cent")
    known_weights = lax.dynamic_update_slice(
        jnp.zeros(block_shape, jnp.float32), cent_weights[:, :, None], (0, 0, own_cent, 0)
    )
    stats = jnp.stack([local_peak.reshape(block_shape), local_total.reshape(block_shape), known_weights])
    stats = merge_stats(stats, ("cent", "sub") if dp_columns else STAGES, {"sub": 1, "dp": 2, "cent": 3})
    weight_float = stats[2].reshape(-1)
    log_sum = (stats[0] + jnp.log(stats[1])).reshape(-1)

    half_log_sum = log_sum.reshape(sizes["sub"], -1)
    half_weight = weight_float.reshape(sizes["sub"], -1)
    centroid_sums = jnp.zeros((own_count, width), jnp.float32)
    own_mass = jnp.zeros((own_count,), jnp.float32)
    for half, rows in enumerate(halves):
        responsibility = (
            half_weight[half][:, None] * jnp.exp(score_blocks[half][0] - half_log_sum[half][:, None])
        ).astype(jnp.bfloat16)
        grouped_resp = responsibility.reshape(sizes["dp"], -1, own_count)
        grouped_rows = rows.reshape(sizes["dp"], -1, width)
        partial_value = lax.dot_general(
            grouped_resp, grouped_rows, (((1,), (1,)), ((0,), (0,))), preferred_element_type=jnp.float32
        ).astype(jnp.bfloat16)
        centroid_sums = centroid_sums + jnp.sum(partial_value.astype(jnp.float32), axis=0)
        weight_mass = jnp.sum(grouped_resp.astype(jnp.float32), axis=1).astype(jnp.bfloat16)
        own_mass = own_mass + jnp.sum(weight_mass.astype(jnp.float32), axis=0)

    moved = own_cents.astype(jnp.float32) + centroid_sums / (own_mass + 1.0)[:, None]
    renormed = normalize(moved).astype(jnp.bfloat16)

    own_log_sum = log_sum.reshape(block_shape)[own_block("sub"), own_block("dp"), own_cent]
    objective = weights.astype(jnp.float32) * own_log_sum / sharpness
    return (centroid_sums, renormed, objective)


def solution(mesh):
    in_specs = (
        P(("groups", "cent", "dp", "sub"), None),
        P(("groups", "cent", "dp", "sub")),
        P(("groups", "cent"), None),
        P(),
    )
    out_specs = (
        P(("groups", "cent", "dp", "sub"), None),
        P(("groups", "cent", "dp", "sub"), None),
        P(("groups", "cent", "dp", "sub")),
    )
    return jax.shard_map(shards, mesh=mesh, in_specs=in_specs, out_specs=out_specs, check_vma=False)
```

```python
import jax
import jax.numpy as jnp
from jax import lax
from jax.sharding import PartitionSpec as P

STAGES = ("cent", "dp", "sub")
SHIFT_MAX = 4


def normalize(values):
    floats = values.astype(jnp.float32)
    return floats * lax.rsqrt(jnp.sum(floats * floats, axis=-1, keepdims=True) + 1e-06)


def relative(name):
    return lax.axis_size(name) <= SHIFT_MAX


def gather_stage(value, name):
    size = lax.axis_size(name)
    if relative(name):
        parts = [value] + [
            lax.ppermute(value, name, [(j, (j + q) % size) for j in range(size)]) for q in range(1, size)
        ]
        return jnp.stack(parts)
    return lax.all_gather(value, name, axis=0)


def own_block(name):
    return 0 if relative(name) else lax.axis_index(name)


def merge_stats(stats, names, block_axis):
    for name in names:
        size = lax.axis_size(name)
        stacked = gather_stage(stats, name)
        if relative(name):
            stacked = jnp.stack([jnp.roll(stacked[q], q, axis=block_axis[name]) for q in range(size)])
        peaks, totals = stacked[:, 0], stacked[:, 1]
        row_peak = jnp.max(peaks, axis=0)
        row_total = jnp.sum(totals * jnp.exp(peaks - row_peak[None]), axis=0)
        stats = jnp.stack([row_peak, row_total, jnp.max(stacked[:, 2], axis=0)])
    return stats


def shards(embeddings, weights, centroids, inverse_temp):
    sharpness = inverse_temp[0]
    row_dev, width = embeddings.shape
    sizes = {name: lax.axis_size(name) for name in STAGES}
    n_groups = sizes["dp"] * sizes["sub"]
    panel = centroids.shape[0]
    own_count = panel // n_groups
    n_rows = row_dev * sizes["cent"] * n_groups
    dp_columns = n_rows * own_count * sizes["dp"] * 4 <= (16 << 20)

    blocks = gather_stage(embeddings, "cent").reshape(-1, width)
    cent_rows = blocks.shape[0]
    weight_block = jnp.pad(weights.astype(jnp.bfloat16)[None, :], ((0, 15), (0, width - row_dev)))
    payload = jnp.concatenate([blocks, weight_block], axis=0)
    for name in STAGES[1:]:
        payload = gather_stage(payload, name)
    halves = [
        normalize(payload[half, :, :cent_rows].reshape(-1, width)).astype(jnp.bfloat16) for half in range(sizes["sub"])
    ]
    cent_weights = payload[:, :, cent_rows, :row_dev].astype(jnp.float32)

    offset = lax.axis_index(("dp", "sub")) * own_count
    if dp_columns:
        dp_index, sub_index = lax.axis_index("dp"), lax.axis_index("sub")
        score_cents = [
            lax.optimization_barrier(
                normalize(
                    lax.dynamic_slice_in_dim(
                        centroids, ((dp_index + q) % sizes["dp"] * sizes["sub"] + sub_index) * own_count, own_count, 0
                    )
                ).astype(jnp.bfloat16)
            )
            for q in range(sizes["dp"])
        ]
    else:
        own_cents = normalize(lax.dynamic_slice_in_dim(centroids, offset, own_count, 0)).astype(jnp.bfloat16)
        score_cents = [lax.optimization_barrier(own_cents)]
    own_cents = score_cents[0]

    score_blocks = [
        [
            lax.dot_general(rows, cents, (((1,), (1,)), ((), ())), preferred_element_type=jnp.float32) * sharpness
            for cents in score_cents
        ]
        for rows in halves
    ]
    block_shape = (sizes["sub"], sizes["dp"], sizes["cent"], row_dev)
    peaks, totals = [], []
    for blocks_of_half in score_blocks:
        half_peak = blocks_of_half[0].max(axis=1)
        for block in blocks_of_half[1:]:
            half_peak = jnp.maximum(half_peak, block.max(axis=1))
        peaks.append(half_peak)
        totals.append(sum(jnp.sum(jnp.exp(block - half_peak[:, None]), axis=1) for block in blocks_of_half))
    local_peak = jnp.concatenate(peaks)
    local_total = jnp.concatenate(totals)

    own_cent = own_block("cent")
    known_weights = lax.dynamic_update_slice(
        jnp.zeros(block_shape, jnp.float32), cent_weights[:, :, None], (0, 0, own_cent, 0)
    )
    stats = jnp.stack([local_peak.reshape(block_shape), local_total.reshape(block_shape), known_weights])
    stats = merge_stats(stats, ("cent", "sub") if dp_columns else STAGES, {"sub": 1, "dp": 2, "cent": 3})
    weight_float = stats[2].reshape(-1)
    log_sum = (stats[0] + jnp.log(stats[1])).reshape(-1)

    if n_rows * width * 2 <= (4 << 20):
        grouped_rows = normalize(payload[:, :, :cent_rows].reshape(-1, width)).astype(jnp.bfloat16)
        grouped_rows = grouped_rows.reshape(n_groups, -1, width)
        own_scores = jnp.concatenate([blocks_of_half[0] for blocks_of_half in score_blocks], axis=0)
        grouped_resp = (
            weight_float[:, None] * jnp.exp(own_scores - log_sum[:, None])
        ).astype(jnp.bfloat16).reshape(n_groups, -1, own_count)
        partial_value = lax.dot_general(
            grouped_resp, grouped_rows, (((1,), (1,)), ((0,), (0,))), preferred_element_type=jnp.float32
        ).astype(jnp.bfloat16)
        centroid_sums = jnp.sum(partial_value.astype(jnp.float32), axis=0)
        weight_mass = jnp.sum(grouped_resp.astype(jnp.float32), axis=1).astype(jnp.bfloat16)
        own_mass = jnp.sum(weight_mass.astype(jnp.float32), axis=0)
    else:
        half_log_sum = log_sum.reshape(sizes["sub"], -1)
        half_weight = weight_float.reshape(sizes["sub"], -1)
        centroid_sums = jnp.zeros((own_count, width), jnp.float32)
        own_mass = jnp.zeros((own_count,), jnp.float32)
        for half, rows in enumerate(halves):
            responsibility = (
                half_weight[half][:, None] * jnp.exp(score_blocks[half][0] - half_log_sum[half][:, None])
            ).astype(jnp.bfloat16)
            grouped_resp = responsibility.reshape(sizes["dp"], -1, own_count)
            grouped_rows = rows.reshape(sizes["dp"], -1, width)
            partial_value = lax.dot_general(
                grouped_resp, grouped_rows, (((1,), (1,)), ((0,), (0,))), preferred_element_type=jnp.float32
            ).astype(jnp.bfloat16)
            centroid_sums = centroid_sums + jnp.sum(partial_value.astype(jnp.float32), axis=0)
            weight_mass = jnp.sum(grouped_resp.astype(jnp.float32), axis=1).astype(jnp.bfloat16)
            own_mass = own_mass + jnp.sum(weight_mass.astype(jnp.float32), axis=0)

    moved = own_cents.astype(jnp.float32) + centroid_sums / (own_mass + 1.0)[:, None]
    renormed = normalize(moved).astype(jnp.bfloat16)

    own_log_sum = log_sum.reshape(block_shape)[own_block("sub"), own_block("dp"), own_cent]
    objective = weights.astype(jnp.float32) * own_log_sum / sharpness
    return (centroid_sums, renormed, objective)


def solution(mesh):
    in_specs = (
        P(("groups", "cent", "dp", "sub"), None),
        P(("groups", "cent", "dp", "sub")),
        P(("groups", "cent"), None),
        P(),
    )
    out_specs = (
        P(("groups", "cent", "dp", "sub"), None),
        P(("groups", "cent", "dp", "sub"), None),
        P(("groups", "cent", "dp", "sub")),
    )
    return jax.shard_map(shards, mesh=mesh, in_specs=in_specs, out_specs=out_specs, check_vma=False)
```

```python
import jax
import jax.numpy as jnp
from jax import lax
from jax.sharding import PartitionSpec as P

STAGES = ("cent", "dp", "sub")
SHIFT_MAX = 4


def normalize(values):
    floats = values.astype(jnp.float32)
    return floats * lax.rsqrt(jnp.sum(floats * floats, axis=-1, keepdims=True) + 1e-06)


def relative(name):
    return lax.axis_size(name) <= SHIFT_MAX


def gather_stage(value, name):
    size = lax.axis_size(name)
    if relative(name):
        parts = [value] + [
            lax.ppermute(value, name, [(j, (j + q) % size) for j in range(size)]) for q in range(1, size)
        ]
        return jnp.stack(parts)
    return lax.all_gather(value, name, axis=0)


def own_block(name):
    return 0 if relative(name) else lax.axis_index(name)


def merge_stats(stats, names, block_axis):
    for name in names:
        size = lax.axis_size(name)
        stacked = gather_stage(stats, name)
        if relative(name):
            stacked = jnp.stack([jnp.roll(stacked[q], q, axis=block_axis[name]) for q in range(size)])
        peaks, totals = stacked[:, 0], stacked[:, 1]
        row_peak = jnp.max(peaks, axis=0)
        row_total = jnp.sum(totals * jnp.exp(peaks - row_peak[None]), axis=0)
        stats = jnp.stack([row_peak, row_total, jnp.max(stacked[:, 2], axis=0)])
    return stats


def shards(embeddings, weights, centroids, inverse_temp):
    sharpness = inverse_temp[0]
    row_dev, width = embeddings.shape
    sizes = {name: lax.axis_size(name) for name in STAGES}
    n_groups = sizes["dp"] * sizes["sub"]
    panel = centroids.shape[0]
    own_count = panel // n_groups
    n_rows = row_dev * sizes["cent"] * n_groups
    dp_columns = n_rows * own_count * sizes["dp"] * 4 <= (16 << 20)

    blocks = gather_stage(embeddings, "cent").reshape(-1, width)
    cent_rows = blocks.shape[0]
    weight_block = jnp.pad(weights.astype(jnp.bfloat16)[None, :], ((0, 15), (0, width - row_dev)))
    payload = jnp.concatenate([blocks, weight_block], axis=0)
    for name in STAGES[1:-1]:
        payload = gather_stage(payload, name)
    payload = jnp.concatenate(
        [normalize(payload[..., :cent_rows, :]).astype(jnp.bfloat16), payload[..., cent_rows:, :]], axis=-2
    )
    payload = gather_stage(payload, STAGES[-1])
    halves = [payload[half, :, :cent_rows].reshape(-1, width) for half in range(sizes["sub"])]
    cent_weights = payload[:, :, cent_rows, :row_dev].astype(jnp.float32)

    offset = lax.axis_index(("dp", "sub")) * own_count
    if dp_columns:
        dp_index, sub_index = lax.axis_index("dp"), lax.axis_index("sub")
        score_cents = [
            lax.optimization_barrier(
                normalize(
                    lax.dynamic_slice_in_dim(
                        centroids, ((dp_index + q) % sizes["dp"] * sizes["sub"] + sub_index) * own_count, own_count, 0
                    )
                ).astype(jnp.bfloat16)
            )
            for q in range(sizes["dp"])
        ]
    else:
        own_cents = normalize(lax.dynamic_slice_in_dim(centroids, offset, own_count, 0)).astype(jnp.bfloat16)
        score_cents = [lax.optimization_barrier(own_cents)]
    own_cents = score_cents[0]

    score_blocks = [
        [
            lax.dot_general(rows, cents, (((1,), (1,)), ((), ())), preferred_element_type=jnp.float32) * sharpness
            for cents in score_cents
        ]
        for rows in halves
    ]
    block_shape = (sizes["sub"], sizes["dp"], sizes["cent"], row_dev)
    peaks, totals = [], []
    for blocks_of_half in score_blocks:
        half_peak = blocks_of_half[0].max(axis=1)
        for block in blocks_of_half[1:]:
            half_peak = jnp.maximum(half_peak, block.max(axis=1))
        peaks.append(half_peak)
        totals.append(sum(jnp.sum(jnp.exp(block - half_peak[:, None]), axis=1) for block in blocks_of_half))
    local_peak = jnp.concatenate(peaks)
    local_total = jnp.concatenate(totals)

    own_cent = own_block("cent")
    known_weights = lax.dynamic_update_slice(
        jnp.zeros(block_shape, jnp.float32), cent_weights[:, :, None], (0, 0, own_cent, 0)
    )
    stats = jnp.stack([local_peak.reshape(block_shape), local_total.reshape(block_shape), known_weights])
    stats = merge_stats(stats, ("cent", "sub") if dp_columns else STAGES, {"sub": 1, "dp": 2, "cent": 3})
    weight_float = stats[2].reshape(-1)
    log_sum = (stats[0] + jnp.log(stats[1])).reshape(-1)

    if n_rows * width * 2 <= (4 << 20):
        grouped_rows = payload[:, :, :cent_rows].reshape(n_groups, -1, width)
        own_scores = jnp.concatenate([blocks_of_half[0] for blocks_of_half in score_blocks], axis=0)
        grouped_resp = (
            weight_float[:, None] * jnp.exp(own_scores - log_sum[:, None])
        ).astype(jnp.bfloat16).reshape(n_groups, -1, own_count)
        partial_value = lax.dot_general(
            grouped_resp, grouped_rows, (((1,), (1,)), ((0,), (0,))), preferred_element_type=jnp.float32
        ).astype(jnp.bfloat16)
        centroid_sums = jnp.sum(partial_value.astype(jnp.float32), axis=0)
        weight_mass = jnp.sum(grouped_resp.astype(jnp.float32), axis=1).astype(jnp.bfloat16)
        own_mass = jnp.sum(weight_mass.astype(jnp.float32), axis=0)
    else:
        half_log_sum = log_sum.reshape(sizes["sub"], -1)
        half_weight = weight_float.reshape(sizes["sub"], -1)
        centroid_sums = jnp.zeros((own_count, width), jnp.float32)
        own_mass = jnp.zeros((own_count,), jnp.float32)
        for half, rows in enumerate(halves):
            responsibility = (
                half_weight[half][:, None] * jnp.exp(score_blocks[half][0] - half_log_sum[half][:, None])
            ).astype(jnp.bfloat16)
            grouped_resp = responsibility.reshape(sizes["dp"], -1, own_count)
            grouped_rows = rows.reshape(sizes["dp"], -1, width)
            partial_value = lax.dot_general(
                grouped_resp, grouped_rows, (((1,), (1,)), ((0,), (0,))), preferred_element_type=jnp.float32
            ).astype(jnp.bfloat16)
            centroid_sums = centroid_sums + jnp.sum(partial_value.astype(jnp.float32), axis=0)
            weight_mass = jnp.sum(grouped_resp.astype(jnp.float32), axis=1).astype(jnp.bfloat16)
            own_mass = own_mass + jnp.sum(weight_mass.astype(jnp.float32), axis=0)

    moved = own_cents.astype(jnp.float32) + centroid_sums / (own_mass + 1.0)[:, None]
    renormed = normalize(moved).astype(jnp.bfloat16)

    own_log_sum = log_sum.reshape(block_shape)[own_block("sub"), own_block("dp"), own_cent]
    objective = weights.astype(jnp.float32) * own_log_sum / sharpness
    return (centroid_sums, renormed, objective)


def solution(mesh):
    in_specs = (
        P(("groups", "cent", "dp", "sub"), None),
        P(("groups", "cent", "dp", "sub")),
        P(("groups", "cent"), None),
        P(),
    )
    out_specs = (
        P(("groups", "cent", "dp", "sub"), None),
        P(("groups", "cent", "dp", "sub"), None),
        P(("groups", "cent", "dp", "sub")),
    )
    return jax.shard_map(shards, mesh=mesh, in_specs=in_specs, out_specs=out_specs, check_vma=False)
```

```python
import jax
import jax.numpy as jnp
from jax import lax
from jax.sharding import PartitionSpec as P

STAGES = ("cent", "dp", "sub")
SHIFT_MAX = 4


def normalize(values):
    floats = values.astype(jnp.float32)
    return floats * lax.rsqrt(jnp.sum(floats * floats, axis=-1, keepdims=True) + 1e-06)


def relative(name):
    return lax.axis_size(name) <= SHIFT_MAX


def gather_stage(value, name):
    size = lax.axis_size(name)
    if relative(name):
        parts = [value] + [
            lax.ppermute(value, name, [(j, (j + q) % size) for j in range(size)]) for q in range(1, size)
        ]
        return jnp.stack(parts)
    return lax.all_gather(value, name, axis=0)


def own_block(name):
    return 0 if relative(name) else lax.axis_index(name)


def merge_stats(stats, names, block_axis):
    for name in names:
        size = lax.axis_size(name)
        stacked = gather_stage(stats, name)
        if relative(name):
            stacked = jnp.stack([jnp.roll(stacked[q], q, axis=block_axis[name]) for q in range(size)])
        peaks, totals = stacked[:, 0], stacked[:, 1]
        row_peak = jnp.max(peaks, axis=0)
        row_total = jnp.sum(totals * jnp.exp(peaks - row_peak[None]), axis=0)
        stats = jnp.stack([row_peak, row_total, jnp.max(stacked[:, 2], axis=0)])
    return stats


def shards(embeddings, weights, centroids, inverse_temp):
    sharpness = inverse_temp[0]
    row_dev, width = embeddings.shape
    sizes = {name: lax.axis_size(name) for name in STAGES}
    n_groups = sizes["dp"] * sizes["sub"]
    panel = centroids.shape[0]
    own_count = panel // n_groups
    n_rows = row_dev * sizes["cent"] * n_groups
    dp_columns = n_rows * own_count * sizes["dp"] * 4 <= (16 << 20)

    blocks = gather_stage(embeddings, "cent").reshape(-1, width)
    cent_rows = blocks.shape[0]
    weight_block = jnp.pad(weights.astype(jnp.bfloat16)[None, :], ((0, 15), (0, width - row_dev)))
    payload = jnp.concatenate([blocks, weight_block], axis=0)
    for name in STAGES[1:-1]:
        payload = gather_stage(payload, name)
    payload = jnp.concatenate(
        [normalize(payload[..., :cent_rows, :]).astype(jnp.bfloat16), payload[..., cent_rows:, :]], axis=-2
    )
    payload = gather_stage(payload, STAGES[-1])
    halves = [payload[half, :, :cent_rows].reshape(-1, width) for half in range(sizes["sub"])]
    cent_weights = payload[:, :, cent_rows, :row_dev].astype(jnp.float32)

    offset = lax.axis_index(("dp", "sub")) * own_count
    if dp_columns:
        dp_index, sub_index = lax.axis_index("dp"), lax.axis_index("sub")
        score_cents = [
            lax.optimization_barrier(
                normalize(
                    lax.dynamic_slice_in_dim(
                        centroids, ((dp_index + q) % sizes["dp"] * sizes["sub"] + sub_index) * own_count, own_count, 0
                    )
                ).astype(jnp.bfloat16)
            )
            for q in range(sizes["dp"])
        ]
    else:
        own_cents = normalize(lax.dynamic_slice_in_dim(centroids, offset, own_count, 0)).astype(jnp.bfloat16)
        score_cents = [lax.optimization_barrier(own_cents)]
    own_cents = score_cents[0]

    score_blocks = [
        [
            lax.dot_general(rows, cents, (((1,), (1,)), ((), ())), preferred_element_type=jnp.float32) * sharpness
            for cents in score_cents
        ]
        for rows in halves
    ]
    block_shape = (sizes["sub"], sizes["dp"], sizes["cent"], row_dev)
    peaks, totals = [], []
    for blocks_of_half in score_blocks:
        half_peak = blocks_of_half[0].max(axis=1)
        for block in blocks_of_half[1:]:
            half_peak = jnp.maximum(half_peak, block.max(axis=1))
        peaks.append(half_peak)
        totals.append(sum(jnp.sum(jnp.exp(block - half_peak[:, None]), axis=1) for block in blocks_of_half))
    local_peak = jnp.concatenate(peaks)
    local_total = jnp.concatenate(totals)

    own_cent = own_block("cent")
    known_weights = lax.dynamic_update_slice(
        jnp.zeros(block_shape, jnp.float32), cent_weights[:, :, None], (0, 0, own_cent, 0)
    )
    stats = jnp.stack([local_peak.reshape(block_shape), local_total.reshape(block_shape), known_weights])
    stats = merge_stats(stats, ("cent", "sub") if dp_columns else STAGES, {"sub": 1, "dp": 2, "cent": 3})
    weight_float = stats[2].reshape(-1)
    log_sum = (stats[0] + jnp.log(stats[1])).reshape(-1)

    if n_rows * width * 2 <= (4 << 20):
        group_shape = (sizes["sub"], sizes["dp"], cent_rows)
        own_scores = jnp.concatenate([blocks_of_half[0] for blocks_of_half in score_blocks], axis=0)
        grouped_resp = (
            weight_float[:, None] * jnp.exp(own_scores - log_sum[:, None])
        ).astype(jnp.bfloat16).reshape(group_shape + (own_count,))
        partial_value = lax.dot_general(
            grouped_resp,
            payload[:, :, :cent_rows],
            (((2,), (2,)), ((0, 1), (0, 1))),
            preferred_element_type=jnp.float32,
        ).astype(jnp.bfloat16)
        centroid_sums = jnp.sum(partial_value.astype(jnp.float32), axis=(0, 1))
        weight_mass = jnp.sum(grouped_resp.astype(jnp.float32), axis=2).astype(jnp.bfloat16)
        own_mass = jnp.sum(weight_mass.astype(jnp.float32), axis=(0, 1))
    else:
        half_log_sum = log_sum.reshape(sizes["sub"], -1)
        half_weight = weight_float.reshape(sizes["sub"], -1)
        centroid_sums = jnp.zeros((own_count, width), jnp.float32)
        own_mass = jnp.zeros((own_count,), jnp.float32)
        for half, rows in enumerate(halves):
            responsibility = (
                half_weight[half][:, None] * jnp.exp(score_blocks[half][0] - half_log_sum[half][:, None])
            ).astype(jnp.bfloat16)
            grouped_resp = responsibility.reshape(sizes["dp"], -1, own_count)
            grouped_rows = rows.reshape(sizes["dp"], -1, width)
            partial_value = lax.dot_general(
                grouped_resp, grouped_rows, (((1,), (1,)), ((0,), (0,))), preferred_element_type=jnp.float32
            ).astype(jnp.bfloat16)
            centroid_sums = centroid_sums + jnp.sum(partial_value.astype(jnp.float32), axis=0)
            weight_mass = jnp.sum(grouped_resp.astype(jnp.float32), axis=1).astype(jnp.bfloat16)
            own_mass = own_mass + jnp.sum(weight_mass.astype(jnp.float32), axis=0)

    moved = own_cents.astype(jnp.float32) + centroid_sums / (own_mass + 1.0)[:, None]
    renormed = normalize(moved).astype(jnp.bfloat16)

    own_log_sum = log_sum.reshape(block_shape)[own_block("sub"), own_block("dp"), own_cent]
    objective = weights.astype(jnp.float32) * own_log_sum / sharpness
    return (centroid_sums, renormed, objective)


def solution(mesh):
    in_specs = (
        P(("groups", "cent", "dp", "sub"), None),
        P(("groups", "cent", "dp", "sub")),
        P(("groups", "cent"), None),
        P(),
    )
    out_specs = (
        P(("groups", "cent", "dp", "sub"), None),
        P(("groups", "cent", "dp", "sub"), None),
        P(("groups", "cent", "dp", "sub")),
    )
    return jax.shard_map(shards, mesh=mesh, in_specs=in_specs, out_specs=out_specs, check_vma=False)
```

```python
import jax
import jax.numpy as jnp
from jax import lax
from jax.sharding import PartitionSpec as P

STAGES = ("cent", "dp", "sub")
SHIFT_MAX = 4


def normalize(values):
    floats = values.astype(jnp.float32)
    return floats * lax.rsqrt(jnp.sum(floats * floats, axis=-1, keepdims=True) + 1e-06)


def relative(name):
    return lax.axis_size(name) <= SHIFT_MAX


def gather_stage(value, name):
    size = lax.axis_size(name)
    if relative(name):
        parts = [value] + [
            lax.ppermute(value, name, [(j, (j + q) % size) for j in range(size)]) for q in range(1, size)
        ]
        return jnp.stack(parts)
    return lax.all_gather(value, name, axis=0)


def own_block(name):
    return 0 if relative(name) else lax.axis_index(name)


def merge_stats(stats, names, block_axis):
    for name in names:
        size = lax.axis_size(name)
        stacked = gather_stage(stats, name)
        if relative(name):
            stacked = jnp.stack([jnp.roll(stacked[q], q, axis=block_axis[name]) for q in range(size)])
        peaks, totals = stacked[:, 0], stacked[:, 1]
        row_peak = jnp.max(peaks, axis=0)
        row_total = jnp.sum(totals * jnp.exp(peaks - row_peak[None]), axis=0)
        stats = jnp.stack([row_peak, row_total, jnp.max(stacked[:, 2], axis=0)])
    return stats


def shards(embeddings, weights, centroids, inverse_temp):
    sharpness = inverse_temp[0]
    row_dev, width = embeddings.shape
    sizes = {name: lax.axis_size(name) for name in STAGES}
    n_groups = sizes["dp"] * sizes["sub"]
    panel = centroids.shape[0]
    own_count = panel // n_groups
    n_rows = row_dev * sizes["cent"] * n_groups
    dp_columns = n_rows * own_count * sizes["dp"] * 4 <= (16 << 20)

    blocks = gather_stage(embeddings, "cent").reshape(-1, width)
    cent_rows = blocks.shape[0]
    weight_block = jnp.pad(weights.astype(jnp.bfloat16)[None, :], ((0, 15), (0, width - row_dev)))
    payload = jnp.concatenate([blocks, weight_block], axis=0)
    for name in STAGES[1:]:
        payload = gather_stage(payload, name)
    halves = [
        normalize(payload[half, :, :cent_rows].reshape(-1, width)).astype(jnp.bfloat16) for half in range(sizes["sub"])
    ]
    cent_weights = payload[:, :, cent_rows, :row_dev].astype(jnp.float32)

    offset = lax.axis_index(("dp", "sub")) * own_count
    if dp_columns:
        dp_index, sub_index = lax.axis_index("dp"), lax.axis_index("sub")
        score_cents = [
            lax.optimization_barrier(
                normalize(
                    lax.dynamic_slice_in_dim(
                        centroids, ((dp_index + q) % sizes["dp"] * sizes["sub"] + sub_index) * own_count, own_count, 0
                    )
                ).astype(jnp.bfloat16)
            )
            for q in range(sizes["dp"])
        ]
    else:
        own_cents = normalize(lax.dynamic_slice_in_dim(centroids, offset, own_count, 0)).astype(jnp.bfloat16)
        score_cents = [lax.optimization_barrier(own_cents)]
    own_cents = score_cents[0]

    score_blocks = [
        [
            lax.dot_general(rows, cents, (((1,), (1,)), ((), ())), preferred_element_type=jnp.float32) * sharpness
            for cents in score_cents
        ]
        for rows in halves
    ]
    block_shape = (sizes["sub"], sizes["dp"], sizes["cent"], row_dev)
    peaks, totals = [], []
    for blocks_of_half in score_blocks:
        half_peak = blocks_of_half[0].max(axis=1)
        for block in blocks_of_half[1:]:
            half_peak = jnp.maximum(half_peak, block.max(axis=1))
        peaks.append(half_peak)
        totals.append(sum(jnp.sum(jnp.exp(block - half_peak[:, None]), axis=1) for block in blocks_of_half))
    local_peak = jnp.concatenate(peaks)
    local_total = jnp.concatenate(totals)

    own_cent = own_block("cent")
    known_weights = lax.dynamic_update_slice(
        jnp.zeros(block_shape, jnp.float32), cent_weights[:, :, None], (0, 0, own_cent, 0)
    )
    stats = jnp.stack([local_peak.reshape(block_shape), local_total.reshape(block_shape), known_weights])
    stats = merge_stats(stats, ("cent", "sub") if dp_columns else STAGES, {"sub": 1, "dp": 2, "cent": 3})
    weight_float = stats[2].reshape(-1)
    log_sum = (stats[0] + jnp.log(stats[1])).reshape(-1)

    if n_rows * width * 2 <= (4 << 20):
        grouped_rows = normalize(payload[:, :, :cent_rows].reshape(-1, width)).astype(jnp.bfloat16)
        grouped_rows = grouped_rows.reshape(n_groups, -1, width)
        own_scores = jnp.concatenate([blocks_of_half[0] for blocks_of_half in score_blocks], axis=0)
        grouped_resp = (
            weight_float[:, None] * jnp.exp(own_scores - log_sum[:, None])
        ).astype(jnp.bfloat16).reshape(n_groups, -1, own_count)
        partial_value = lax.dot_general(
            grouped_resp, grouped_rows, (((1,), (1,)), ((0,), (0,))), preferred_element_type=jnp.float32
        ).astype(jnp.bfloat16)
        centroid_sums = jnp.sum(partial_value.astype(jnp.float32), axis=0)
        weight_mass = jnp.sum(grouped_resp.astype(jnp.float32), axis=1).astype(jnp.bfloat16)
        own_mass = jnp.sum(weight_mass.astype(jnp.float32), axis=0)
    else:
        half_log_sum = log_sum.reshape(sizes["sub"], -1)
        half_weight = weight_float.reshape(sizes["sub"], -1)
        centroid_sums = jnp.zeros((own_count, width), jnp.float32)
        own_mass = jnp.zeros((own_count,), jnp.float32)
        for half, rows in enumerate(halves):
            responsibility = (
                half_weight[half][:, None] * jnp.exp(score_blocks[half][0] - half_log_sum[half][:, None])
            ).astype(jnp.bfloat16)
            grouped_resp = responsibility.reshape(sizes["dp"], -1, own_count)
            grouped_rows = rows.reshape(sizes["dp"], -1, width)
            partial_value = lax.dot_general(
                grouped_resp, grouped_rows, (((1,), (1,)), ((0,), (0,))), preferred_element_type=jnp.float32
            ).astype(jnp.bfloat16)
            centroid_sums = centroid_sums + jnp.sum(partial_value.astype(jnp.float32), axis=0)
            weight_mass = jnp.sum(grouped_resp.astype(jnp.float32), axis=1).astype(jnp.bfloat16)
            own_mass = own_mass + jnp.sum(weight_mass.astype(jnp.float32), axis=0)

    moved = own_cents.astype(jnp.float32) + centroid_sums / (own_mass + 1.0)[:, None]
    renormed = normalize(moved).astype(jnp.bfloat16)

    own_rows = (own_block("sub"), own_block("dp"), own_cent)
    objective = (weight_float.reshape(block_shape)[own_rows] * log_sum.reshape(block_shape)[own_rows]) / sharpness
    return (centroid_sums, renormed, objective)


def solution(mesh):
    in_specs = (
        P(("groups", "cent", "dp", "sub"), None),
        P(("groups", "cent", "dp", "sub")),
        P(("groups", "cent"), None),
        P(),
    )
    out_specs = (
        P(("groups", "cent", "dp", "sub"), None),
        P(("groups", "cent", "dp", "sub"), None),
        P(("groups", "cent", "dp", "sub")),
    )
    return jax.shard_map(shards, mesh=mesh, in_specs=in_specs, out_specs=out_specs, check_vma=False)
```

```python
import jax
import jax.numpy as jnp
from jax import lax
from jax.sharding import PartitionSpec as P

STAGES = ("cent", "dp", "sub")
SHIFT_MAX = 4


def normalize(values):
    floats = values.astype(jnp.float32)
    return floats * lax.rsqrt(jnp.sum(floats * floats, axis=-1, keepdims=True) + 1e-06)


def relative(name):
    return lax.axis_size(name) <= SHIFT_MAX


def gather_stage(value, name):
    size = lax.axis_size(name)
    if relative(name):
        parts = [value] + [
            lax.ppermute(value, name, [(j, (j + q) % size) for j in range(size)]) for q in range(1, size)
        ]
        return jnp.stack(parts)
    return lax.all_gather(value, name, axis=0)


def own_block(name):
    return 0 if relative(name) else lax.axis_index(name)


def merge_stats(stats, names, block_axis):
    for name in names:
        size = lax.axis_size(name)
        stacked = gather_stage(stats, name)
        if relative(name):
            stacked = jnp.stack([jnp.roll(stacked[q], q, axis=block_axis[name]) for q in range(size)])
        peaks, totals = stacked[:, 0], stacked[:, 1]
        row_peak = jnp.max(peaks, axis=0)
        row_total = jnp.sum(totals * jnp.exp(peaks - row_peak[None]), axis=0)
        stats = jnp.stack([row_peak, row_total, jnp.max(stacked[:, 2], axis=0)])
    return stats


def shards(embeddings, weights, centroids, inverse_temp):
    sharpness = inverse_temp[0]
    row_dev, width = embeddings.shape
    sizes = {name: lax.axis_size(name) for name in STAGES}
    n_groups = sizes["dp"] * sizes["sub"]
    panel = centroids.shape[0]
    own_count = panel // n_groups
    n_rows = row_dev * sizes["cent"] * n_groups
    dp_columns = n_rows * own_count * sizes["dp"] * 4 <= (16 << 20)

    blocks = gather_stage(embeddings, "cent").reshape(-1, width)
    cent_rows = blocks.shape[0]
    weight_block = jnp.pad(weights.astype(jnp.bfloat16)[None, :], ((0, 15), (0, width - row_dev)))
    payload = jnp.concatenate([blocks, weight_block], axis=0)
    for name in STAGES[1:]:
        payload = gather_stage(payload, name)
    halves = [
        normalize(payload[half, :, :cent_rows].reshape(-1, width)).astype(jnp.bfloat16) for half in range(sizes["sub"])
    ]
    cent_weights = payload[:, :, cent_rows, :row_dev].astype(jnp.float32)

    offset = lax.axis_index(("dp", "sub")) * own_count
    if dp_columns:
        dp_index, sub_index = lax.axis_index("dp"), lax.axis_index("sub")
        score_cents = [
            lax.optimization_barrier(
                normalize(
                    lax.dynamic_slice_in_dim(
                        centroids, ((dp_index + q) % sizes["dp"] * sizes["sub"] + sub_index) * own_count, own_count, 0
                    )
                ).astype(jnp.bfloat16)
            )
            for q in range(sizes["dp"])
        ]
    else:
        own_cents = normalize(lax.dynamic_slice_in_dim(centroids, offset, own_count, 0)).astype(jnp.bfloat16)
        score_cents = [lax.optimization_barrier(own_cents)]
    own_cents = score_cents[0]

    score_blocks = [
        [
            lax.dot_general(rows, cents, (((1,), (1,)), ((), ())), preferred_element_type=jnp.float32) * sharpness
            for cents in score_cents
        ]
        for rows in halves
    ]
    block_shape = (sizes["sub"], sizes["dp"], sizes["cent"], row_dev)
    peaks, totals = [], []
    for blocks_of_half in score_blocks:
        half_peak = blocks_of_half[0].max(axis=1)
        for block in blocks_of_half[1:]:
            half_peak = jnp.maximum(half_peak, block.max(axis=1))
        peaks.append(half_peak)
        totals.append(sum(jnp.sum(jnp.exp(block - half_peak[:, None]), axis=1) for block in blocks_of_half))
    local_peak = jnp.concatenate(peaks)
    local_total = jnp.concatenate(totals)

    own_cent = own_block("cent")
    known_weights = lax.dynamic_update_slice(
        jnp.zeros(block_shape, jnp.float32), cent_weights[:, :, None], (0, 0, own_cent, 0)
    )
    stats = jnp.stack([local_peak.reshape(block_shape), local_total.reshape(block_shape), known_weights])
    stats = merge_stats(stats, ("cent", "sub") if dp_columns else STAGES, {"sub": 1, "dp": 2, "cent": 3})
    weight_float = stats[2].reshape(-1)
    log_sum = (stats[0] + jnp.log(stats[1])).reshape(-1)

    if n_rows * width * 2 <= (4 << 20):
        grouped_rows = jnp.concatenate(halves, axis=0).reshape(n_groups, -1, width)
        own_scores = jnp.concatenate([blocks_of_half[0] for blocks_of_half in score_blocks], axis=0)
        grouped_resp = (
            weight_float[:, None] * jnp.exp(own_scores - log_sum[:, None])
        ).astype(jnp.bfloat16).reshape(n_groups, -1, own_count)
        partial_value = lax.dot_general(
            grouped_resp, grouped_rows, (((1,), (1,)), ((0,), (0,))), preferred_element_type=jnp.float32
        ).astype(jnp.bfloat16)
        centroid_sums = jnp.sum(partial_value.astype(jnp.float32), axis=0)
        weight_mass = jnp.sum(grouped_resp.astype(jnp.float32), axis=1).astype(jnp.bfloat16)
        own_mass = jnp.sum(weight_mass.astype(jnp.float32), axis=0)
    else:
        half_log_sum = log_sum.reshape(sizes["sub"], -1)
        half_weight = weight_float.reshape(sizes["sub"], -1)
        centroid_sums = jnp.zeros((own_count, width), jnp.float32)
        own_mass = jnp.zeros((own_count,), jnp.float32)
        for half, rows in enumerate(halves):
            responsibility = (
                half_weight[half][:, None] * jnp.exp(score_blocks[half][0] - half_log_sum[half][:, None])
            ).astype(jnp.bfloat16)
            grouped_resp = responsibility.reshape(sizes["dp"], -1, own_count)
            grouped_rows = rows.reshape(sizes["dp"], -1, width)
            partial_value = lax.dot_general(
                grouped_resp, grouped_rows, (((1,), (1,)), ((0,), (0,))), preferred_element_type=jnp.float32
            ).astype(jnp.bfloat16)
            centroid_sums = centroid_sums + jnp.sum(partial_value.astype(jnp.float32), axis=0)
            weight_mass = jnp.sum(grouped_resp.astype(jnp.float32), axis=1).astype(jnp.bfloat16)
            own_mass = own_mass + jnp.sum(weight_mass.astype(jnp.float32), axis=0)

    moved = own_cents.astype(jnp.float32) + centroid_sums / (own_mass + 1.0)[:, None]
    renormed = normalize(moved).astype(jnp.bfloat16)

    own_log_sum = log_sum.reshape(block_shape)[own_block("sub"), own_block("dp"), own_cent]
    objective = weights.astype(jnp.float32) * own_log_sum / sharpness
    return (centroid_sums, renormed, objective)


def solution(mesh):
    in_specs = (
        P(("groups", "cent", "dp", "sub"), None),
        P(("groups", "cent", "dp", "sub")),
        P(("groups", "cent"), None),
        P(),
    )
    out_specs = (
        P(("groups", "cent", "dp", "sub"), None),
        P(("groups", "cent", "dp", "sub"), None),
        P(("groups", "cent", "dp", "sub")),
    )
    return jax.shard_map(shards, mesh=mesh, in_specs=in_specs, out_specs=out_specs, check_vma=False)
```
